512 devices in a mesh: replica: 64 (over z, x), shard: 8 (over y, core).
Axes of the slice: x: 4, y: 4, z: 16, core: 2. Of those that a mesh axis runs over, the one named last changes fastest.
Arguments:
- grad_query: float32 [512, 512, 384], P(('replica', 'shard')), may hold values from -1.25 to 1.25
- grad_output: float32 [512, 384, 512], P(('replica', 'shard')), may hold values from -1.25 to 1.25
- grad_norm: float32 [512, 512], P(('replica', 'shard')), may hold values from -1.25 to 1.25
- grad_bias: float32 [512, 32, 6], P(('replica', 'shard')), may hold values from -0.3 to 0.3
- weight_query: float32 [512, 384], P('shard'), may hold values from -5.303301 to 5.303301
- weight_output: float32 [384, 512], P('shard'), may hold values from -6.1237244 to 6.1237244
- weight_norm: float32 [512], P('shard'), may hold values from 0 to 120
- weight_bias: float32 [32, 6], P('shard'), may hold values from -120 to 120
- first_query: float32 [512, 384], P('shard'), may hold values from -120 to 120
- first_output: float32 [384, 512], P('shard'), may hold values from -120 to 120
- first_norm: float32 [512], P('shard'), may hold values from -120 to 120
- first_bias: float32 [32, 6], P('shard'), may hold values from -120 to 120
- second_query: float32 [512, 384], P('shard'), may hold values from 0.05 to 2
- second_output: float32 [384, 512], P('shard'), may hold values from 0.05 to 2
- second_norm: float32 [512], P('shard'), may hold values from 0.05 to 2
- second_bias: float32 [32, 6], P('shard'), may hold values from 0.05 to 2
Outputs:
- updated_query: bfloat16 [512, 384], replicated
- updated_output: bfloat16 [384, 512], replicated
- updated_norm: bfloat16 [512], replicated
- updated_bias: bfloat16 [32, 6], replicated
- first_query_next: float32 [512, 384], P('shard')
- first_output_next: float32 [384, 512], P('shard')
- first_norm_next: float32 [512], P('shard')
- first_bias_next: float32 [32, 6], P('shard')
- second_query_next: float32 [512, 384], P('shard')
- second_output_next: float32 [384, 512], P('shard')
- second_norm_next: float32 [512], P('shard')
- second_bias_next: float32 [32, 6], P('shard')
- norm_table: float32 [2, 4], replicated
- trust_ratios: float32 [4], replicated
The draws below stay inside these ranges and needn't reach their ends.
All inputs are finite; a program needn't handle non-finite values.
Results may differ from the reference program's by a relative error of at most 0.008.
Values may be sent and summed in bfloat16 or wider, within the bound.
No kernel may reach another device: no remote copies, remote signals or barrier semaphores. Data moves between devices by JAX's collectives and lax.ppermute only.
A program may use at most 64 MiB of HBM per device.

```python
import math
import jax
import jax.numpy as jnp
from jax import lax

D = 512
HEADS = 6
BUCKETS = 32
INNER = 384
DEVICES = 512


def scaled_draw(key, row_count, column_count, factor, label):
    folded = jax.random.fold_in(key, label)
    subkeys = jax.random.split(folded, 3)
    row_scale = jnp.exp(jax.random.uniform(subkeys[1], (row_count, 1), jnp.float32) * math.log(10.0))
    column_scale = jnp.exp(jax.random.uniform(subkeys[2], (1, column_count), jnp.float32) * math.log(10.0))
    trend = jnp.exp(0.5 * math.log(3.0) * jnp.arange(row_count, dtype=jnp.float32) / row_count)[:, None]
    base = jax.random.normal(subkeys[0], (row_count, column_count), jnp.float32)
    base = jnp.clip(base, -4.0, 4.0)
    return base * row_scale * column_scale * trend * factor


def draw_weight_query(key, part):
    return scaled_draw(key, D, INNER, 0.1 / math.sqrt(D), 11)


def draw_weight_output(key, part):
    return scaled_draw(key, INNER, D, 0.1 / math.sqrt(INNER), 12)


def draw_weight_norm(key, part):
    return jnp.abs(scaled_draw(key, D, 1, 0.1, 13))[:, 0]


def draw_weight_bias(key, part):
    return scaled_draw(key, BUCKETS, HEADS, 0.1, 14)


def draw_first_query(key, part):
    return scaled_draw(key, D, INNER, 0.1, 15)


def draw_first_output(key, part):
    return scaled_draw(key, INNER, D, 0.1, 16)


def draw_first_norm(key, part):
    return scaled_draw(key, D, 1, 0.1, 17)[:, 0]


def draw_first_bias(key, part):
    return scaled_draw(key, BUCKETS, HEADS, 0.1, 18)


def strengthened(result, key, source, target, shards_of, factor):
    def block_of(dim):
        return (jnp.arange(result.shape[dim]) // (result.shape[dim] // shards_of)).reshape((-1,) + (1,) * (result.ndim - 1 - dim))

    one_side = jax.random.permutation(key, shards_of)[block_of(target)]
    other_side = (block_of(target) + shards_of // 2) % shards_of
    return jnp.where((block_of(source) == one_side) | (block_of(source) == other_side), factor * result, result)


def level_of(own_key, dims, pieces, smallest, top_value):
    gain, own = 1.0, jax.random.fold_in(own_key, 6)
    for dim, blocks in pieces:
        heights = jnp.exp(jax.random.uniform(jax.random.fold_in(own, dim), (blocks,), jnp.float32, smallest / len(pieces), top_value / len(pieces)))
        gain = gain * jnp.repeat(heights, dims[dim] // blocks).reshape([-1 if axis == dim else 1 for axis in range(len(dims))])
    return gain


def noise_with(own_key, shape, scale, bound, cuts, heavy, kind=jnp.bfloat16):
    values = scale * jax.random.normal(own_key, shape, jnp.float32)
    if cuts:
        values = values * level_of(own_key, shape, cuts, -0.22, 0.18)
    return jnp.clip(strengthened(values, jax.random.fold_in(own_key, 3), *heavy), -bound, bound).astype(kind)


def setup_inputs(seed: int = 0) -> dict:
    seeds = jax.random.split(jax.random.key(seed), 17)
    return {
        "grad_query": noise_with(seeds[0], (DEVICES, D, INNER), 0.05, 1.25, ((0, 512),), (0, 1, 512, 6.0), jnp.float32),
        "grad_output": noise_with(seeds[1], (DEVICES, INNER, D), 0.05, 1.25, ((0, 512),), (0, 1, 128, 5.5), jnp.float32),
        "grad_norm": noise_with(seeds[2], (DEVICES, D), 0.05, 1.25, ((0, 512),), (0, 1, 512, 6.0), jnp.float32),
        "grad_bias": noise_with(seeds[3], (DEVICES, BUCKETS, HEADS), 0.05, 0.3, ((0, 512),), (0, 1, 32, 2.75), jnp.float32),
        "weight_query": draw_weight_query(jax.random.fold_in(seeds[16], 71), 0),
        "weight_output": draw_weight_output(jax.random.fold_in(seeds[16], 71), 0),
        "weight_norm": draw_weight_norm(jax.random.fold_in(seeds[16], 71), 0),
        "weight_bias": draw_weight_bias(jax.random.fold_in(seeds[16], 71), 0),
        "first_query": draw_first_query(jax.random.fold_in(seeds[16], 71), 0),
        "first_output": draw_first_output(jax.random.fold_in(seeds[16], 71), 0),
        "first_norm": draw_first_norm(jax.random.fold_in(seeds[16], 71), 0),
        "first_bias": draw_first_bias(jax.random.fold_in(seeds[16], 71), 0),
        "second_query": jnp.clip(jnp.exp(math.log(2.0) - 3.6888794 * jax.random.uniform(seeds[12], (D, INNER), jnp.float32) ** level_of(seeds[12], (D, INNER), ((0, 8),), -0.2, 0.2)), 0.05, 2.0),
        "second_output": jnp.clip(jnp.exp(math.log(2.0) - 3.6888794 * jax.random.uniform(seeds[13], (INNER, D), jnp.float32) ** level_of(seeds[13], (INNER, D), ((0, 8),), -0.2, 0.2)), 0.05, 2.0),
        "second_norm": jnp.clip(jnp.exp(math.log(2.0) - 3.6888794 * jax.random.uniform(seeds[14], (D,), jnp.float32) ** level_of(seeds[14], (D,), ((0, 8),), -0.2, 0.2)), 0.05, 2.0),
        "second_bias": jnp.clip(jnp.exp(math.log(2.0) - 3.6888794 * jax.random.uniform(seeds[15], (BUCKETS, HEADS), jnp.float32) ** level_of(seeds[15], (BUCKETS, HEADS), ((0, 8),), -0.2, 0.2)), 0.05, 2.0),
    }


def lamb_piece(gradient, moment, second, weight, decay_rate):
    summed = lax.optimization_barrier(jnp.sum(gradient, axis=0))
    moment_next = 0.5 * moment + 0.5 * summed
    second_next = 0.5 * second + 0.5 * summed * summed
    update = moment_next / (jnp.sqrt(second_next) + 1e-06) + decay_rate * weight
    weight_size = jnp.sqrt(jnp.sum(weight * weight))
    update_size = jnp.sqrt(jnp.sum(update * update))
    ratio = weight_size / (update_size + 1e-06)
    updated = (weight - 0.01 * ratio * update).astype(jnp.bfloat16)
    return (updated, moment_next, second_next, weight_size, update_size, ratio)

def reference(grad_query, grad_output, grad_norm, grad_bias, weight_query, weight_output, weight_norm, weight_bias, first_query, first_output, first_norm, first_bias, second_query, second_output, second_norm, second_bias):
    query_out = lamb_piece(grad_query, first_query, second_query, weight_query, 0.01)
    output_out = lamb_piece(grad_output, first_output, second_output, weight_output, 0.01)
    norm_out = lamb_piece(grad_norm, first_norm, second_norm, weight_norm, 0.0)
    bias_out = lamb_piece(grad_bias, first_bias, second_bias, weight_bias, 0.0)
    listed = [query_out, output_out, norm_out, bias_out]
    weight_sizes = jnp.stack([entry[3] for entry in listed])
    update_sizes = jnp.stack([entry[4] for entry in listed])
    norm_table = jnp.stack([weight_sizes, update_sizes])
    trust_ratios = jnp.stack([entry[5] for entry in listed])
    return (query_out[0], output_out[0], norm_out[0], bias_out[0], query_out[1], output_out[1], norm_out[1], bias_out[1], query_out[2], output_out[2], norm_out[2], bias_out[2], norm_table, trust_ratios)
```

```python
import jax
import jax.numpy as jnp
from jax import lax
from jax.sharding import PartitionSpec as P

LANES = 128
SHARD_BITS = (0, 1, 2)
REPLICA_BITS = (3, 5, 4, 6, 7, 8)
AXES = ("replica", "shard")


def step_math(summed, moment, second, weight, decay_rate):
    moment_next = 0.5 * moment + 0.5 * summed
    second_next = 0.5 * second + 0.5 * summed * summed
    update = moment_next / (jnp.sqrt(second_next) + 1e-06) + decay_rate * weight
    return (moment_next, second_next, update)


def padded_width(width, multiple):
    return -(-width // multiple) * multiple


def bit_of(index, bit):
    return (index >> bit) & 1


def exchange(value, bit, devices):
    return lax.ppermute(value, AXES, [(d, d ^ (1 << bit)) for d in range(devices)])


def halve(rows, bits, devices):
    index = lax.axis_index(AXES)
    for bit in bits:
        half = rows.shape[0] // 2
        mine = bit_of(index, bit)
        keep = lax.dynamic_slice_in_dim(rows, mine * half, half, 0)
        send = lax.dynamic_slice_in_dim(rows, (1 - mine) * half, half, 0)
        rows = keep + exchange(send, bit, devices)
    return rows


def double(rows, bits, devices):
    index = lax.axis_index(AXES)
    for bit in reversed(bits):
        other = exchange(rows, bit, devices)
        first = bit_of(index, bit) == 0
        rows = jnp.concatenate([jnp.where(first, rows, other), jnp.where(first, other, rows)], axis=0)
    return rows


def on_device(
    grad_query,
    grad_output,
    grad_norm,
    grad_bias,
    weight_query,
    weight_output,
    weight_norm,
    weight_bias,
    first_query,
    first_output,
    first_norm,
    first_bias,
    second_query,
    second_output,
    second_norm,
    second_bias,
    shards,
    replicas,
):
    weights = (weight_query, weight_output, weight_norm, weight_bias)
    moments = (first_query, first_output, first_norm, first_bias)
    seconds = (second_query, second_output, second_norm, second_bias)
    decay_rates = (0.01, 0.01, 0.0, 0.0)
    gradients = (grad_query[0], grad_output[0], grad_norm[0], grad_bias[0])
    sizes = [weight.size for weight in weights]
    offsets = [sum(sizes[:member]) for member in range(4)]
    total = sum(sizes)
    devices = shards * replicas
    width = padded_width(total, LANES * replicas)
    levels = len(SHARD_BITS)
    position = [sum(((s >> SHARD_BITS[j]) & 1) << (levels - 1 - j) for j in range(levels)) for s in range(shards)]
    blocks = [gradient.reshape(shards, -1) for gradient in gradients]
    filler = jnp.zeros((width - total,), jnp.float32)
    packed = jnp.stack(
        [jnp.concatenate([block[position.index(p)] for block in blocks] + [filler]) for p in range(shards)]
    )
    chunks = packed.reshape(shards * replicas * (width // replicas // LANES), LANES)
    mine = halve(chunks, SHARD_BITS + REPLICA_BITS, devices)
    block = double(mine, REPLICA_BITS, devices)
    summed_flat = block.reshape(width)
    summed_all = [
        summed_flat[offsets[member] : offsets[member] + sizes[member]].reshape(weights[member].shape)
        for member in range(4)
    ]
    results = [
        step_math(
            summed_all[member],
            moments[member],
            seconds[member],
            weights[member],
            decay_rates[member],
        )
        for member in range(4)
    ]
    weight_squares = [jnp.sum(weight * weight) for weight in weights]
    update_squares = [jnp.sum(result[2] * result[2]) for result in results]
    squares = lax.psum(jnp.stack(weight_squares + update_squares), "shard")
    weight_sizes = jnp.sqrt(squares[:4])
    update_sizes = jnp.sqrt(squares[4:])
    trust_ratios = weight_sizes / (update_sizes + 1e-06)
    shards_out = [
        (weights[member] - 0.01 * trust_ratios[member] * results[member][2]).astype(jnp.bfloat16).reshape(-1)
        for member in range(4)
    ]
    out_width = padded_width(total, LANES)
    shards_out.append(jnp.zeros((out_width - total,), jnp.bfloat16))
    gathered = lax.all_gather(jnp.concatenate(shards_out), "shard", axis=0, tiled=False)
    full = [
        gathered[:, offsets[member] : offsets[member] + sizes[member]].reshape(
            (shards * weights[member].shape[0],) + weights[member].shape[1:]
        )
        for member in range(4)
    ]
    norm_table = jnp.stack([weight_sizes, update_sizes])
    return (
        full[0],
        full[1],
        full[2],
        full[3],
        results[0][0],
        results[1][0],
        results[2][0],
        results[3][0],
        results[0][1],
        results[1][1],
        results[2][1],
        results[3][1],
        norm_table,
        trust_ratios,
    )


def solution(mesh):
    shards = mesh.shape["shard"]
    replicas = mesh.shape["replica"]
    placed = (
        P(("replica", "shard"), None, None),
        P(("replica", "shard"), None, None),
        P(("replica", "shard"), None),
        P(("replica", "shard"), None, None),
        P("shard", None),
        P("shard", None),
        P("shard"),
        P("shard", None),
        P("shard", None),
        P("shard", None),
        P("shard"),
        P("shard", None),
        P("shard", None),
        P("shard", None),
        P("shard"),
        P("shard", None),
    )

    def body(*args):
        return on_device(*args, shards=shards, replicas=replicas)

    return jax.shard_map(
        body,
        mesh=mesh,
        in_specs=placed,
        out_specs=(
            P(),
            P(),
            P(),
            P(),
            P("shard", None),
            P("shard", None),
            P("shard"),
            P("shard", None),
            P("shard", None),
            P("shard", None),
            P("shard"),
            P("shard", None),
            P(),
            P(),
        ),
        check_vma=False,
    )
```

```python
import jax
import jax.numpy as jnp
from jax import lax
from jax.sharding import PartitionSpec as P

LANES = 128
SHARD_GROUPS = ((0,), (1, 2))
REPLICA_GROUPS = ((3, 5), (4, 6), (7, 8))
AXES = ("replica", "shard")


def step_math(summed, moment, second, weight, decay_rate):
    moment_next = 0.5 * moment + 0.5 * summed
    second_next = 0.5 * second + 0.5 * summed * summed
    update = moment_next / (jnp.sqrt(second_next) + 1e-06) + decay_rate * weight
    return (moment_next, second_next, update)


def padded_width(width, multiple):
    return -(-width // multiple) * multiple


def bit_of(index, bit):
    return (index >> bit) & 1


def exchange(value, mask, devices):
    return lax.ppermute(value, AXES, [(d, d ^ mask) for d in range(devices)])


def masks_of(group):
    width = len(group)
    return [
        sum(((t >> (width - 1 - j)) & 1) << group[j] for j in range(width))
        for t in range(1 << width)
    ]


def part_of(index, group):
    return sum(bit_of(index, bit) << (len(group) - 1 - j) for j, bit in enumerate(group))


def halve(rows, groups, devices):
    index = lax.axis_index(AXES)
    for group in groups:
        count = 1 << len(group)
        size = rows.shape[0] // count
        mine = part_of(index, group)
        masks = masks_of(group)
        total = lax.dynamic_slice_in_dim(rows, mine * size, size, 0)
        for t in range(1, count):
            part = lax.dynamic_slice_in_dim(rows, (mine ^ t) * size, size, 0)
            total = total + exchange(part, masks[t], devices)
        rows = total
    return rows


def double(rows, groups, devices):
    index = lax.axis_index(AXES)
    for group in reversed(groups):
        count = 1 << len(group)
        mine = part_of(index, group)
        masks = masks_of(group)
        got = [rows] + [exchange(rows, masks[t], devices) for t in range(1, count)]
        ordered = []
        for j in range(count):
            owner = mine ^ j
            pick = got[0]
            for t in range(1, count):
                pick = jnp.where(owner == t, got[t], pick)
            ordered.append(pick)
        rows = jnp.concatenate(ordered, axis=0)
    return rows


def on_device(
    grad_query,
    grad_output,
    grad_norm,
    grad_bias,
    weight_query,
    weight_output,
    weight_norm,
    weight_bias,
    first_query,
    first_output,
    first_norm,
    first_bias,
    second_query,
    second_output,
    second_norm,
    second_bias,
    shards,
    replicas,
):
    weights = (weight_query, weight_output, weight_norm, weight_bias)
    moments = (first_query, first_output, first_norm, first_bias)
    seconds = (second_query, second_output, second_norm, second_bias)
    decay_rates = (0.01, 0.01, 0.0, 0.0)
    gradients = (grad_query[0], grad_output[0], grad_norm[0], grad_bias[0])
    sizes = [weight.size for weight in weights]
    offsets = [sum(sizes[:member]) for member in range(4)]
    total = sum(sizes)
    devices = shards * replicas
    width = padded_width(total, LANES * replicas)
    rows = [gradient.reshape(shards, -1) for gradient in gradients]
    rows.append(jnp.zeros((shards, width - total), jnp.float32))
    packed = jnp.concatenate(rows, axis=1)
    levels = shards.bit_length() - 1
    packed = packed.reshape((2,) * levels + (width,))
    packed = packed.transpose(tuple(reversed(range(levels))) + (levels,))
    chunks = packed.reshape(shards * replicas * (width // replicas // LANES), LANES)
    mine = halve(chunks, SHARD_GROUPS + REPLICA_GROUPS, devices)
    block = double(mine, REPLICA_GROUPS, devices)
    summed_flat = block.reshape(width)
    summed_all = [
        summed_flat[offsets[member] : offsets[member] + sizes[member]].reshape(weights[member].shape)
        for member in range(4)
    ]
    results = [
        step_math(
            summed_all[member],
            moments[member],
            seconds[member],
            weights[member],
            decay_rates[member],
        )
        for member in range(4)
    ]
    weight_squares = [jnp.sum(weight * weight) for weight in weights]
    update_squares = [jnp.sum(result[2] * result[2]) for result in results]
    squares = lax.psum(jnp.stack(weight_squares + update_squares), "shard")
    weight_sizes = jnp.sqrt(squares[:4])
    update_sizes = jnp.sqrt(squares[4:])
    trust_ratios = weight_sizes / (update_sizes + 1e-06)
    shards_out = [
        (weights[member] - 0.01 * trust_ratios[member] * results[member][2]).astype(jnp.bfloat16).reshape(-1)
        for member in range(4)
    ]
    out_width = padded_width(total, LANES)
    shards_out.append(jnp.zeros((out_width - total,), jnp.bfloat16))
    gathered = lax.all_gather(jnp.concatenate(shards_out), "shard", axis=0, tiled=False)
    full = [
        gathered[:, offsets[member] : offsets[member] + sizes[member]].reshape(
            (shards * weights[member].shape[0],) + weights[member].shape[1:]
        )
        for member in range(4)
    ]
    norm_table = jnp.stack([weight_sizes, update_sizes])
    return (
        full[0],
        full[1],
        full[2],
        full[3],
        results[0][0],
        results[1][0],
        results[2][0],
        results[3][0],
        results[0][1],
        results[1][1],
        results[2][1],
        results[3][1],
        norm_table,
        trust_ratios,
    )


def solution(mesh):
    shards = mesh.shape["shard"]
    replicas = mesh.shape["replica"]
    placed = (
        P(("replica", "shard"), None, None),
        P(("replica", "shard"), None, None),
        P(("replica", "shard"), None),
        P(("replica", "shard"), None, None),
        P("shard", None),
        P("shard", None),
        P("shard"),
        P("shard", None),
        P("shard", None),
        P("shard", None),
        P("shard"),
        P("shard", None),
        P("shard", None),
        P("shard", None),
        P("shard"),
        P("shard", None),
    )

    def body(*args):
        return on_device(*args, shards=shards, replicas=replicas)

    return jax.shard_map(
        body,
        mesh=mesh,
        in_specs=placed,
        out_specs=(
            P(),
            P(),
            P(),
            P(),
            P("shard", None),
            P("shard", None),
            P("shard"),
            P("shard", None),
            P("shard", None),
            P("shard", None),
            P("shard"),
            P("shard", None),
            P(),
            P(),
        ),
        check_vma=False,
    )
```

```python
import jax
import jax.numpy as jnp
from jax import lax
from jax.sharding import PartitionSpec as P

LANES = 128
CORE_BIT = 0
Y_GROUP = (2, 1)
REPLICA_BITS = (3, 5, 4, 6, 7, 8)
AXES = ("replica", "shard")


def step_math(summed, moment, second, weight, decay_rate):
    moment_next = 0.5 * moment + 0.5 * summed
    second_next = 0.5 * second + 0.5 * summed * summed
    update = moment_next / (jnp.sqrt(second_next) + 1e-06) + decay_rate * weight
    return (moment_next, second_next, update)


def padded_width(width, multiple):
    return -(-width // multiple) * multiple


def bit_of(index, bit):
    return (index >> bit) & 1


def exchange(value, mask, devices):
    return lax.ppermute(value, AXES, [(d, d ^ mask) for d in range(devices)])


def masks_of(group):
    width = len(group)
    return [
        sum(((t >> (width - 1 - j)) & 1) << group[j] for j in range(width))
        for t in range(1 << width)
    ]


def part_of(index, group):
    return sum(bit_of(index, bit) << (len(group) - 1 - j) for j, bit in enumerate(group))


def reduce_blocks(packed, devices):
    index = lax.axis_index(AXES)
    shards = packed.shape[0]
    pairs = packed.reshape((shards // 2, 2) + packed.shape[1:])
    mine = bit_of(index, CORE_BIT)
    keep = lax.dynamic_index_in_dim(pairs, mine, 1, keepdims=False)
    send = lax.dynamic_index_in_dim(pairs, 1 - mine, 1, keepdims=False)
    blocks = keep + exchange(send, 1 << CORE_BIT, devices)
    mine = part_of(index, Y_GROUP)
    masks = masks_of(Y_GROUP)
    total = lax.dynamic_index_in_dim(blocks, mine, 0, keepdims=False)
    for t in range(1, len(masks)):
        part = lax.dynamic_index_in_dim(blocks, mine ^ t, 0, keepdims=False)
        total = total + exchange(part, masks[t], devices)
    for bit in REPLICA_BITS:
        total = total + exchange(total, 1 << bit, devices)
    return total


def on_device(
    grad_query,
    grad_output,
    grad_norm,
    grad_bias,
    weight_query,
    weight_output,
    weight_norm,
    weight_bias,
    first_query,
    first_output,
    first_norm,
    first_bias,
    second_query,
    second_output,
    second_norm,
    second_bias,
    shards,
    replicas,
):
    weights = (weight_query, weight_output, weight_norm, weight_bias)
    moments = (first_query, first_output, first_norm, first_bias)
    seconds = (second_query, second_output, second_norm, second_bias)
    decay_rates = (0.01, 0.01, 0.0, 0.0)
    gradients = (grad_query[0], grad_output[0], grad_norm[0], grad_bias[0])
    sizes = [weight.size for weight in weights]
    offsets = [sum(sizes[:member]) for member in range(4)]
    total = sum(sizes)
    devices = shards * replicas
    query_rows, lanes = weight_query.shape
    output_rows = weight_output.size // lanes
    small = jnp.concatenate(
        [grad_norm[0].reshape(shards, -1), grad_bias[0].reshape(shards, -1)], axis=1
    )
    small_width = small.shape[1]
    small = jnp.pad(small, ((0, 0), (0, lanes - small_width))).reshape(shards, 1, lanes)
    small = jnp.pad(small, ((0, 0), (0, 7), (0, 0)))
    packed = jnp.concatenate(
        [
            grad_query[0].reshape(shards, query_rows, lanes),
            grad_output[0].reshape(shards, output_rows, lanes),
            small,
        ],
        axis=1,
    )
    block = reduce_blocks(packed, devices)
    summed_rest = block[query_rows + output_rows, :small_width]
    summed_all = [
        block[:query_rows],
        block[query_rows : query_rows + output_rows].reshape(weight_output.shape),
        summed_rest[: weight_norm.size].reshape(weight_norm.shape),
        summed_rest[weight_norm.size :].reshape(weight_bias.shape),
    ]
    results = [
        step_math(
            summed_all[member],
            moments[member],
            seconds[member],
            weights[member],
            decay_rates[member],
        )
        for member in range(4)
    ]
    weight_squares = [jnp.sum(weight * weight) for weight in weights]
    update_squares = [jnp.sum(result[2] * result[2]) for result in results]
    squares = lax.psum(tuple(weight_squares + update_squares), "shard")
    weight_sizes = jnp.sqrt(jnp.stack(squares[:4]))
    update_sizes = jnp.sqrt(jnp.stack(squares[4:]))
    trust_ratios = weight_sizes / (update_sizes + 1e-06)
    shards_out = [
        (weights[member] - 0.01 * trust_ratios[member] * results[member][2]).astype(jnp.bfloat16).reshape(-1)
        for member in range(4)
    ]
    out_width = padded_width(total, LANES)
    shards_out.append(jnp.zeros((out_width - total,), jnp.bfloat16))
    gathered = lax.all_gather(jnp.concatenate(shards_out), "shard", axis=0, tiled=False)
    full = [
        gathered[:, offsets[member] : offsets[member] + sizes[member]].reshape(
            (shards * weights[member].shape[0],) + weights[member].shape[1:]
        )
        for member in range(4)
    ]
    norm_table = jnp.stack([weight_sizes, update_sizes])
    return (
        full[0],
        full[1],
        full[2],
        full[3],
        results[0][0],
        results[1][0],
        results[2][0],
        results[3][0],
        results[0][1],
        results[1][1],
        results[2][1],
        results[3][1],
        norm_table,
        trust_ratios,
    )


def solution(mesh):
    shards = mesh.shape["shard"]
    replicas = mesh.shape["replica"]
    placed = (
        P(("replica", "shard"), None, None),
        P(("replica", "shard"), None, None),
        P(("replica", "shard"), None),
        P(("replica", "shard"), None, None),
        P("shard", None),
        P("shard", None),
        P("shard"),
        P("shard", None),
        P("shard", None),
        P("shard", None),
        P("shard"),
        P("shard", None),
        P("shard", None),
        P("shard", None),
        P("shard"),
        P("shard", None),
    )

    def body(*args):
        return on_device(*args, shards=shards, replicas=replicas)

    return jax.shard_map(
        body,
        mesh=mesh,
        in_specs=placed,
        out_specs=(
            P(),
            P(),
            P(),
            P(),
            P("shard", None),
            P("shard", None),
            P("shard"),
            P("shard", None),
            P("shard", None),
            P("shard", None),
            P("shard"),
            P("shard", None),
            P(),
            P(),
        ),
        check_vma=False,
    )
```

```python
import jax
import jax.numpy as jnp
from jax import lax
from jax.sharding import PartitionSpec as P

LANES = 128
CORE_BIT = 0
Y_GROUP = (2, 1)
REPLICA_SPLIT_BITS = (3, 5)
REPLICA_BUTTERFLY_BITS = (4, 6, 7, 8)
ROW_TILE = 8
AXES = ("replica", "shard")


def step_math(summed, moment, second, weight, decay_rate):
    moment_next = 0.5 * moment + 0.5 * summed
    second_next = 0.5 * second + 0.5 * summed * summed
    update = moment_next / (jnp.sqrt(second_next) + 1e-06) + decay_rate * weight
    return (moment_next, second_next, update)


def padded_width(width, multiple):
    return -(-width // multiple) * multiple


def bit_of(index, bit):
    return (index >> bit) & 1


def exchange(value, mask, devices):
    return lax.ppermute(value, AXES, [(d, d ^ mask) for d in range(devices)])


def masks_of(group):
    width = len(group)
    return [
        sum(((t >> (width - 1 - j)) & 1) << group[j] for j in range(width))
        for t in range(1 << width)
    ]


def part_of(index, group):
    return sum(bit_of(index, bit) << (len(group) - 1 - j) for j, bit in enumerate(group))


def reduce_blocks(packed, devices):
    index = lax.axis_index(AXES)
    shards = packed.shape[0]
    pairs = packed.reshape((shards // 2, 2) + packed.shape[1:])
    mine = bit_of(index, CORE_BIT)
    keep = lax.dynamic_index_in_dim(pairs, mine, 1, keepdims=False)
    send = lax.dynamic_index_in_dim(pairs, 1 - mine, 1, keepdims=False)
    blocks = keep + exchange(send, 1 << CORE_BIT, devices)
    mine = part_of(index, Y_GROUP)
    masks = masks_of(Y_GROUP)
    total = lax.dynamic_index_in_dim(blocks, mine, 0, keepdims=False)
    for t in range(1, len(masks)):
        part = lax.dynamic_index_in_dim(blocks, mine ^ t, 0, keepdims=False)
        total = total + exchange(part, masks[t], devices)
    rows, lanes = total.shape
    multiple = ROW_TILE << len(REPLICA_SPLIT_BITS)
    total = jnp.pad(total, ((0, padded_width(rows, multiple) - rows), (0, 0)))
    for bit in REPLICA_SPLIT_BITS:
        halves = total.reshape((2, total.shape[0] // 2, lanes))
        mine = bit_of(index, bit)
        keep = lax.dynamic_index_in_dim(halves, mine, 0, keepdims=False)
        send = lax.dynamic_index_in_dim(halves, 1 - mine, 0, keepdims=False)
        total = keep + exchange(send, 1 << bit, devices)
    for bit in REPLICA_BUTTERFLY_BITS:
        total = total + exchange(total, 1 << bit, devices)
    for bit in reversed(REPLICA_SPLIT_BITS):
        other = exchange(total, 1 << bit, devices)
        first = bit_of(index, bit) == 0
        total = jnp.concatenate([jnp.where(first, total, other), jnp.where(first, other, total)], axis=0)
    return total[:rows]


def on_device(
    grad_query,
    grad_output,
    grad_norm,
    grad_bias,
    weight_query,
    weight_output,
    weight_norm,
    weight_bias,
    first_query,
    first_output,
    first_norm,
    first_bias,
    second_query,
    second_output,
    second_norm,
    second_bias,
    shards,
    replicas,
):
    weights = (weight_query, weight_output, weight_norm, weight_bias)
    moments = (first_query, first_output, first_norm, first_bias)
    seconds = (second_query, second_output, second_norm, second_bias)
    decay_rates = (0.01, 0.01, 0.0, 0.0)
    gradients = (grad_query[0], grad_output[0], grad_norm[0], grad_bias[0])
    sizes = [weight.size for weight in weights]
    offsets = [sum(sizes[:member]) for member in range(4)]
    total = sum(sizes)
    devices = shards * replicas
    query_rows, lanes = weight_query.shape
    output_rows = weight_output.size // lanes
    small = jnp.concatenate(
        [grad_norm[0].reshape(shards, -1), grad_bias[0].reshape(shards, -1)], axis=1
    )
    small_width = small.shape[1]
    small = jnp.pad(small, ((0, 0), (0, lanes - small_width))).reshape(shards, 1, lanes)
    small = jnp.pad(small, ((0, 0), (0, 7), (0, 0)))
    packed = jnp.concatenate(
        [
            grad_query[0].reshape(shards, query_rows, lanes),
            grad_output[0].reshape(shards, output_rows, lanes),
            small,
        ],
        axis=1,
    )
    block = reduce_blocks(packed, devices)
    summed_rest = block[query_rows + output_rows, :small_width]
    summed_all = [
        block[:query_rows],
        block[query_rows : query_rows + output_rows].reshape(weight_output.shape),
        summed_rest[: weight_norm.size].reshape(weight_norm.shape),
        summed_rest[weight_norm.size :].reshape(weight_bias.shape),
    ]
    results = [
        step_math(
            summed_all[member],
            moments[member],
            seconds[member],
            weights[member],
            decay_rates[member],
        )
        for member in range(4)
    ]
    weight_squares = [jnp.sum(weight * weight) for weight in weights]
    update_squares = [jnp.sum(result[2] * result[2]) for result in results]
    squares = lax.psum(tuple(weight_squares + update_squares), "shard")
    weight_sizes = jnp.sqrt(jnp.stack(squares[:4]))
    update_sizes = jnp.sqrt(jnp.stack(squares[4:]))
    trust_ratios = weight_sizes / (update_sizes + 1e-06)
    shards_out = [
        (weights[member] - 0.01 * trust_ratios[member] * results[member][2]).astype(jnp.bfloat16).reshape(-1)
        for member in range(4)
    ]
    out_width = padded_width(total, LANES)
    shards_out.append(jnp.zeros((out_width - total,), jnp.bfloat16))
    gathered = lax.all_gather(jnp.concatenate(shards_out), "shard", axis=0, tiled=False)
    full = [
        gathered[:, offsets[member] : offsets[member] + sizes[member]].reshape(
            (shards * weights[member].shape[0],) + weights[member].shape[1:]
        )
        for member in range(4)
    ]
    norm_table = jnp.stack([weight_sizes, update_sizes])
    return (
        full[0],
        full[1],
        full[2],
        full[3],
        results[0][0],
        results[1][0],
        results[2][0],
        results[3][0],
        results[0][1],
        results[1][1],
        results[2][1],
        results[3][1],
        norm_table,
        trust_ratios,
    )


def solution(mesh):
    shards = mesh.shape["shard"]
    replicas = mesh.shape["replica"]
    placed = (
        P(("replica", "shard"), None, None),
        P(("replica", "shard"), None, None),
        P(("replica", "shard"), None),
        P(("replica", "shard"), None, None),
        P("shard", None),
        P("shard", None),
        P("shard"),
        P("shard", None),
        P("shard", None),
        P("shard", None),
        P("shard"),
        P("shard", None),
        P("shard", None),
        P("shard", None),
        P("shard"),
        P("shard", None),
    )

    def body(*args):
        return on_device(*args, shards=shards, replicas=replicas)

    return jax.shard_map(
        body,
        mesh=mesh,
        in_specs=placed,
        out_specs=(
            P(),
            P(),
            P(),
            P(),
            P("shard", None),
            P("shard", None),
            P("shard"),
            P("shard", None),
            P("shard", None),
            P("shard", None),
            P("shard"),
            P("shard", None),
            P(),
            P(),
        ),
        check_vma=False,
    )
```

```python
import jax
import jax.numpy as jnp
from jax import lax
from jax.sharding import PartitionSpec as P

LANES = 128
CORE_BIT = 0
Y_GROUP = (2, 1)
REPLICA_SPLIT_BITS = (3, 5)
REPLICA_BUTTERFLY_BITS = (4, 6, 7, 8)
ROW_TILE = 8
AXES = ("replica", "shard")


def step_math(summed, moment, second, weight, decay_rate):
    moment_next = 0.5 * moment + 0.5 * summed
    second_next = 0.5 * second + 0.5 * summed * summed
    update = moment_next / (jnp.sqrt(second_next) + 1e-06) + decay_rate * weight
    return (moment_next, second_next, update)


def padded_width(width, multiple):
    return -(-width // multiple) * multiple


def bit_of(index, bit):
    return (index >> bit) & 1


def exchange(value, mask, devices):
    return lax.ppermute(value, AXES, [(d, d ^ mask) for d in range(devices)])


def masks_of(group):
    width = len(group)
    return [
        sum(((t >> (width - 1 - j)) & 1) << group[j] for j in range(width))
        for t in range(1 << width)
    ]


def part_of(index, group):
    return sum(bit_of(index, bit) << (len(group) - 1 - j) for j, bit in enumerate(group))


def reduce_blocks(packed, devices):
    index = lax.axis_index(AXES)
    shards = packed.shape[0]
    pairs = packed.reshape((shards // 2, 2) + packed.shape[1:])
    mine = bit_of(index, CORE_BIT)
    keep = lax.dynamic_index_in_dim(pairs, mine, 1, keepdims=False)
    send = lax.dynamic_index_in_dim(pairs, 1 - mine, 1, keepdims=False)
    blocks = keep + exchange(send, 1 << CORE_BIT, devices)
    mine = part_of(index, Y_GROUP)
    masks = masks_of(Y_GROUP)
    total = lax.dynamic_index_in_dim(blocks, mine, 0, keepdims=False)
    for t in range(1, len(masks)):
        part = lax.dynamic_index_in_dim(blocks, mine ^ t, 0, keepdims=False)
        total = total + exchange(part, masks[t], devices)
    rows, lanes = total.shape
    multiple = ROW_TILE << len(REPLICA_SPLIT_BITS)
    total = jnp.pad(total, ((0, padded_width(rows, multiple) - rows), (0, 0)))
    for bit in REPLICA_SPLIT_BITS:
        halves = total.reshape((2, total.shape[0] // 2, lanes))
        mine = bit_of(index, bit)
        keep = lax.dynamic_index_in_dim(halves, mine, 0, keepdims=False)
        send = lax.dynamic_index_in_dim(halves, 1 - mine, 0, keepdims=False)
        total = keep + exchange(send, 1 << bit, devices)
    for bit in REPLICA_BUTTERFLY_BITS:
        total = total + exchange(total, 1 << bit, devices)
    for bit in reversed(REPLICA_SPLIT_BITS):
        other = exchange(total, 1 << bit, devices)
        first = bit_of(index, bit) == 0
        total = jnp.concatenate([jnp.where(first, total, other), jnp.where(first, other, total)], axis=0)
    return total[:rows]


def as_tile(value, rows, lanes):
    if value.size == rows * lanes:
        return value.reshape(rows, lanes)
    flat = value.reshape(1, -1)
    flat = jnp.pad(flat, ((0, 0), (0, lanes * (-(-flat.shape[1] // lanes)) - flat.shape[1])))
    flat = flat.reshape(-1, lanes)
    return jnp.pad(flat, ((0, rows - flat.shape[0]), (0, 0)))


def on_device(
    grad_query,
    grad_output,
    grad_norm,
    grad_bias,
    weight_query,
    weight_output,
    weight_norm,
    weight_bias,
    first_query,
    first_output,
    first_norm,
    first_bias,
    second_query,
    second_output,
    second_norm,
    second_bias,
    shards,
    replicas,
):
    weights = (weight_query, weight_output, weight_norm, weight_bias)
    moments = (first_query, first_output, first_norm, first_bias)
    seconds = (second_query, second_output, second_norm, second_bias)
    decay_rates = (0.01, 0.01, 0.0, 0.0)
    gradients = (grad_query[0], grad_output[0], grad_norm[0], grad_bias[0])
    sizes = [weight.size for weight in weights]
    offsets = [sum(sizes[:member]) for member in range(4)]
    total = sum(sizes)
    devices = shards * replicas
    query_rows, lanes = weight_query.shape
    output_rows = weight_output.size // lanes
    small = jnp.concatenate(
        [grad_norm[0].reshape(shards, -1), grad_bias[0].reshape(shards, -1)], axis=1
    )
    small_width = small.shape[1]
    small = jnp.pad(small, ((0, 0), (0, lanes - small_width))).reshape(shards, 1, lanes)
    small = jnp.pad(small, ((0, 0), (0, 7), (0, 0)))
    packed = jnp.concatenate(
        [
            grad_query[0].reshape(shards, query_rows, lanes),
            grad_output[0].reshape(shards, output_rows, lanes),
            small,
        ],
        axis=1,
    )
    block = reduce_blocks(packed, devices)
    summed_rest = block[query_rows + output_rows, :small_width]
    summed_all = [
        block[:query_rows],
        block[query_rows : query_rows + output_rows].reshape(weight_output.shape),
        summed_rest[: weight_norm.size].reshape(weight_norm.shape),
        summed_rest[weight_norm.size :].reshape(weight_bias.shape),
    ]
    results = [
        step_math(
            summed_all[member],
            moments[member],
            seconds[member],
            weights[member],
            decay_rates[member],
        )
        for member in range(4)
    ]
    terms = [as_tile(weight, query_rows, lanes) for weight in weights]
    terms += [as_tile(result[2], query_rows, lanes) for result in results]
    stacked = jnp.stack(terms)
    squares = lax.psum(jnp.sum(stacked * stacked, axis=(1, 2)), "shard")
    weight_sizes = jnp.sqrt(squares[:4])
    update_sizes = jnp.sqrt(squares[4:])
    trust_ratios = weight_sizes / (update_sizes + 1e-06)
    shards_out = [
        (weights[member] - 0.01 * trust_ratios[member] * results[member][2]).astype(jnp.bfloat16).reshape(-1)
        for member in range(4)
    ]
    out_width = padded_width(total, LANES)
    shards_out.append(jnp.zeros((out_width - total,), jnp.bfloat16))
    gathered = lax.all_gather(jnp.concatenate(shards_out), "shard", axis=0, tiled=False)
    full = [
        gathered[:, offsets[member] : offsets[member] + sizes[member]].reshape(
            (shards * weights[member].shape[0],) + weights[member].shape[1:]
        )
        for member in range(4)
    ]
    norm_table = jnp.stack([weight_sizes, update_sizes])
    return (
        full[0],
        full[1],
        full[2],
        full[3],
        results[0][0],
        results[1][0],
        results[2][0],
        results[3][0],
        results[0][1],
        results[1][1],
        results[2][1],
        results[3][1],
        norm_table,
        trust_ratios,
    )


def solution(mesh):
    shards = mesh.shape["shard"]
    replicas = mesh.shape["replica"]
    placed = (
        P(("replica", "shard"), None, None),
        P(("replica", "shard"), None, None),
        P(("replica", "shard"), None),
        P(("replica", "shard"), None, None),
        P("shard", None),
        P("shard", None),
        P("shard"),
        P("shard", None),
        P("shard", None),
        P("shard", None),
        P("shard"),
        P("shard", None),
        P("shard", None),
        P("shard", None),
        P("shard"),
        P("shard", None),
    )

    def body(*args):
        return on_device(*args, shards=shards, replicas=replicas)

    return jax.shard_map(
        body,
        mesh=mesh,
        in_specs=placed,
        out_specs=(
            P(),
            P(),
            P(),
            P(),
            P("shard", None),
            P("shard", None),
            P("shard"),
            P("shard", None),
            P("shard", None),
            P("shard", None),
            P("shard"),
            P("shard", None),
            P(),
            P(),
        ),
        check_vma=False,
    )
```

```python
import jax
import jax.numpy as jnp
from jax import lax
from jax.sharding import PartitionSpec as P

LANES = 128
CORE_BIT = 0
Y_GROUP = (2, 1)
REPLICA_SPLITS = ((0b11 << 3, 4), (1 << 5, 5))
REPLICA_BUTTERFLY = (1 << 3, 1 << 6, 1 << 7, 0b11 << 7)
ROW_TILE = 8
AXES = ("replica", "shard")


def step_math(summed, moment, second, weight, decay_rate):
    moment_next = 0.5 * moment + 0.5 * summed
    second_next = 0.5 * second + 0.5 * summed * summed
    update = moment_next / (jnp.sqrt(second_next) + 1e-06) + decay_rate * weight
    return (moment_next, second_next, update)


def padded_width(width, multiple):
    return -(-width // multiple) * multiple


def bit_of(index, bit):
    return (index >> bit) & 1


def exchange(value, mask, devices):
    return lax.ppermute(value, AXES, [(d, d ^ mask) for d in range(devices)])


def masks_of(group):
    width = len(group)
    return [
        sum(((t >> (width - 1 - j)) & 1) << group[j] for j in range(width))
        for t in range(1 << width)
    ]


def part_of(index, group):
    return sum(bit_of(index, bit) << (len(group) - 1 - j) for j, bit in enumerate(group))


def reduce_blocks(packed, devices):
    index = lax.axis_index(AXES)
    shards = packed.shape[0]
    pairs = packed.reshape((shards // 2, 2) + packed.shape[1:])
    mine = bit_of(index, CORE_BIT)
    keep = lax.dynamic_index_in_dim(pairs, mine, 1, keepdims=False)
    send = lax.dynamic_index_in_dim(pairs, 1 - mine, 1, keepdims=False)
    blocks = keep + exchange(send, 1 << CORE_BIT, devices)
    mine = part_of(index, Y_GROUP)
    masks = masks_of(Y_GROUP)
    total = lax.dynamic_index_in_dim(blocks, mine, 0, keepdims=False)
    for t in range(1, len(masks)):
        part = lax.dynamic_index_in_dim(blocks, mine ^ t, 0, keepdims=False)
        total = total + exchange(part, masks[t], devices)
    rows, lanes = total.shape
    multiple = ROW_TILE << len(REPLICA_SPLITS)
    total = jnp.pad(total, ((0, padded_width(rows, multiple) - rows), (0, 0)))
    for mask, bit in REPLICA_SPLITS:
        halves = total.reshape((2, total.shape[0] // 2, lanes))
        mine = bit_of(index, bit)
        keep = lax.dynamic_index_in_dim(halves, mine, 0, keepdims=False)
        send = lax.dynamic_index_in_dim(halves, 1 - mine, 0, keepdims=False)
        total = keep + exchange(send, mask, devices)
    for mask in REPLICA_BUTTERFLY:
        total = total + exchange(total, mask, devices)
    for mask, bit in reversed(REPLICA_SPLITS):
        other = exchange(total, mask, devices)
        first = bit_of(index, bit) == 0
        total = jnp.concatenate([jnp.where(first, total, other), jnp.where(first, other, total)], axis=0)
    return total[:rows]


def as_tile(value, rows, lanes):
    if value.size == rows * lanes:
        return value.reshape(rows, lanes)
    flat = value.reshape(1, -1)
    flat = jnp.pad(flat, ((0, 0), (0, lanes * (-(-flat.shape[1] // lanes)) - flat.shape[1])))
    flat = flat.reshape(-1, lanes)
    return jnp.pad(flat, ((0, rows - flat.shape[0]), (0, 0)))


def on_device(
    grad_query,
    grad_output,
    grad_norm,
    grad_bias,
    weight_query,
    weight_output,
    weight_norm,
    weight_bias,
    first_query,
    first_output,
    first_norm,
    first_bias,
    second_query,
    second_output,
    second_norm,
    second_bias,
    shards,
    replicas,
):
    weights = (weight_query, weight_output, weight_norm, weight_bias)
    moments = (first_query, first_output, first_norm, first_bias)
    seconds = (second_query, second_output, second_norm, second_bias)
    decay_rates = (0.01, 0.01, 0.0, 0.0)
    gradients = (grad_query[0], grad_output[0], grad_norm[0], grad_bias[0])
    sizes = [weight.size for weight in weights]
    offsets = [sum(sizes[:member]) for member in range(4)]
    total = sum(sizes)
    devices = shards * replicas
    query_rows, lanes = weight_query.shape
    output_rows = weight_output.size // lanes
    small = jnp.concatenate(
        [grad_norm[0].reshape(shards, -1), grad_bias[0].reshape(shards, -1)], axis=1
    )
    small_width = small.shape[1]
    small = jnp.pad(small, ((0, 0), (0, lanes - small_width))).reshape(shards, 1, lanes)
    small = jnp.pad(small, ((0, 0), (0, 7), (0, 0)))
    packed = jnp.concatenate(
        [
            grad_query[0].reshape(shards, query_rows, lanes),
            grad_output[0].reshape(shards, output_rows, lanes),
            small,
        ],
        axis=1,
    )
    block = reduce_blocks(packed, devices)
    summed_rest = block[query_rows + output_rows, :small_width]
    summed_all = [
        block[:query_rows],
        block[query_rows : query_rows + output_rows].reshape(weight_output.shape),
        summed_rest[: weight_norm.size].reshape(weight_norm.shape),
        summed_rest[weight_norm.size :].reshape(weight_bias.shape),
    ]
    results = [
        step_math(
            summed_all[member],
            moments[member],
            seconds[member],
            weights[member],
            decay_rates[member],
        )
        for member in range(4)
    ]
    terms = [as_tile(weight, query_rows, lanes) for weight in weights]
    terms += [as_tile(result[2], query_rows, lanes) for result in results]
    stacked = jnp.stack(terms)
    squares = lax.psum(jnp.sum(stacked * stacked, axis=(1, 2)), "shard")
    weight_sizes = jnp.sqrt(squares[:4])
    update_sizes = jnp.sqrt(squares[4:])
    trust_ratios = weight_sizes / (update_sizes + 1e-06)
    shards_out = [
        (weights[member] - 0.01 * trust_ratios[member] * results[member][2]).astype(jnp.bfloat16).reshape(-1)
        for member in range(4)
    ]
    out_width = padded_width(total, LANES)
    shards_out.append(jnp.zeros((out_width - total,), jnp.bfloat16))
    gathered = lax.all_gather(jnp.concatenate(shards_out), "shard", axis=0, tiled=False)
    full = [
        gathered[:, offsets[member] : offsets[member] + sizes[member]].reshape(
            (shards * weights[member].shape[0],) + weights[member].shape[1:]
        )
        for member in range(4)
    ]
    norm_table = jnp.stack([weight_sizes, update_sizes])
    return (
        full[0],
        full[1],
        full[2],
        full[3],
        results[0][0],
        results[1][0],
        results[2][0],
        results[3][0],
        results[0][1],
        results[1][1],
        results[2][1],
        results[3][1],
        norm_table,
        trust_ratios,
    )


def solution(mesh):
    shards = mesh.shape["shard"]
    replicas = mesh.shape["replica"]
    placed = (
        P(("replica", "shard"), None, None),
        P(("replica", "shard"), None, None),
        P(("replica", "shard"), None),
        P(("replica", "shard"), None, None),
        P("shard", None),
        P("shard", None),
        P("shard"),
        P("shard", None),
        P("shard", None),
        P("shard", None),
        P("shard"),
        P("shard", None),
        P("shard", None),
        P("shard", None),
        P("shard"),
        P("shard", None),
    )

    def body(*args):
        return on_device(*args, shards=shards, replicas=replicas)

    return jax.shard_map(
        body,
        mesh=mesh,
        in_specs=placed,
        out_specs=(
            P(),
            P(),
            P(),
            P(),
            P("shard", None),
            P("shard", None),
            P("shard"),
            P("shard", None),
            P("shard", None),
            P("shard", None),
            P("shard"),
            P("shard", None),
            P(),
            P(),
        ),
        check_vma=False,
    )
```

```python
import jax
import jax.numpy as jnp
from jax import lax
from jax.sharding import PartitionSpec as P

LANES = 128
CORE_BIT = 0
Y_GROUP = (2, 1)
REPLICA_SPLITS = ((0b11 << 3, 4), (1 << 5, 5))
REPLICA_BUTTERFLY = (1 << 3, 1 << 6, 1 << 7, 0b11 << 7)
ROW_TILE = 8
AXES = ("replica", "shard")


def step_math(summed, moment, second, weight, decay_rate):
    moment_next = 0.5 * moment + 0.5 * summed
    second_next = 0.5 * second + 0.5 * summed * summed
    update = moment_next / (jnp.sqrt(second_next) + 1e-06) + decay_rate * weight
    return (moment_next, second_next, update)


def padded_width(width, multiple):
    return -(-width // multiple) * multiple


def bit_of(index, bit):
    return (index >> bit) & 1


def exchange(value, mask, devices):
    return lax.ppermute(value, AXES, [(d, d ^ mask) for d in range(devices)])


def masks_of(group):
    width = len(group)
    return [
        sum(((t >> (width - 1 - j)) & 1) << group[j] for j in range(width))
        for t in range(1 << width)
    ]


def part_of(index, group):
    return sum(bit_of(index, bit) << (len(group) - 1 - j) for j, bit in enumerate(group))


def reduce_blocks(packed, devices):
    index = lax.axis_index(AXES)
    shards = packed.shape[0]
    pairs = packed.reshape((shards // 2, 2) + packed.shape[1:])
    mine = bit_of(index, CORE_BIT)
    keep = lax.dynamic_index_in_dim(pairs, mine, 1, keepdims=False)
    send = lax.dynamic_index_in_dim(pairs, 1 - mine, 1, keepdims=False)
    blocks = keep + exchange(send, 1 << CORE_BIT, devices)
    mine = part_of(index, Y_GROUP)
    masks = masks_of(Y_GROUP)
    total = lax.dynamic_index_in_dim(blocks, mine, 0, keepdims=False)
    for t in range(1, len(masks)):
        part = lax.dynamic_index_in_dim(blocks, mine ^ t, 0, keepdims=False)
        total = total + exchange(part, masks[t], devices)
    rows, lanes = total.shape
    multiple = ROW_TILE << len(REPLICA_SPLITS)
    total = jnp.pad(total, ((0, padded_width(rows, multiple) - rows), (0, 0)))
    for mask, bit in REPLICA_SPLITS:
        halves = total.reshape((2, total.shape[0] // 2, lanes))
        mine = bit_of(index, bit)
        keep = lax.dynamic_index_in_dim(halves, mine, 0, keepdims=False)
        send = lax.dynamic_index_in_dim(halves, 1 - mine, 0, keepdims=False)
        total = keep + exchange(send, mask, devices)
    for mask in REPLICA_BUTTERFLY:
        total = total + exchange(total, mask, devices)
    for mask, bit in reversed(REPLICA_SPLITS):
        other = exchange(total, mask, devices)
        first = bit_of(index, bit) == 0
        total = jnp.concatenate([jnp.where(first, total, other), jnp.where(first, other, total)], axis=0)
    return total[:rows]


def pack(query, output, norm, bias, rows, pad_rows):
    lanes = query.shape[-1]
    rest = jnp.concatenate([norm.reshape(-1), bias.reshape(-1)])
    rest = jnp.pad(rest, (0, lanes - rest.shape[0])).reshape(1, lanes)
    block = jnp.concatenate([query, output.reshape(-1, lanes), rest], axis=0)
    return jnp.pad(block, ((0, pad_rows - block.shape[0]), (0, 0)))


def unpack(block, shapes):
    query_shape, output_shape, norm_shape, bias_shape = shapes
    query_rows, lanes = query_shape
    output_rows = (output_shape[0] * output_shape[1]) // lanes
    norm_size = norm_shape[0]
    bias_size = bias_shape[0] * bias_shape[1]
    rest = block[..., query_rows + output_rows, :]
    return (
        block[..., :query_rows, :],
        block[..., query_rows : query_rows + output_rows, :],
        rest[..., :norm_size],
        rest[..., norm_size : norm_size + bias_size],
    )


def on_device(
    grad_query,
    grad_output,
    grad_norm,
    grad_bias,
    weight_query,
    weight_output,
    weight_norm,
    weight_bias,
    first_query,
    first_output,
    first_norm,
    first_bias,
    second_query,
    second_output,
    second_norm,
    second_bias,
    shards,
    replicas,
):
    devices = shards * replicas
    shapes = (weight_query.shape, weight_output.shape, weight_norm.shape, weight_bias.shape)
    query_rows, lanes = weight_query.shape
    output_rows = weight_output.size // lanes
    block_rows = padded_width(query_rows + output_rows + 1, ROW_TILE)
    packed = jax.vmap(lambda q, o, n, b: pack(q, o, n, b, query_rows + output_rows + 1, block_rows))(
        grad_query[0].reshape(shards, query_rows, lanes),
        grad_output[0].reshape(shards, -1, weight_output.shape[1]),
        grad_norm[0].reshape(shards, -1),
        grad_bias[0].reshape(shards, -1),
    )
    summed = reduce_blocks(packed, devices)
    weight = pack(weight_query, weight_output, weight_norm, weight_bias, block_rows, block_rows)
    moment = pack(first_query, first_output, first_norm, first_bias, block_rows, block_rows)
    second = pack(second_query, second_output, second_norm, second_bias, block_rows, block_rows)
    row = lax.broadcasted_iota(jnp.int32, (block_rows, lanes), 0)
    lane = lax.broadcasted_iota(jnp.int32, (block_rows, lanes), 1)
    norm_size = weight_norm.size
    bias_size = weight_bias.size
    member = jnp.where(
        row < query_rows,
        0,
        jnp.where(
            row < query_rows + output_rows,
            1,
            jnp.where(
                row == query_rows + output_rows,
                jnp.where(lane < norm_size, 2, jnp.where(lane < norm_size + bias_size, 3, 4)),
                4,
            ),
        ),
    )
    decay_rate = jnp.where(member < 2, 0.01, 0.0).astype(jnp.float32)
    moment_next, second_next, update = step_math(summed, moment, second, weight, decay_rate)
    members = jnp.arange(4, dtype=jnp.int32).reshape(4, 1, 1)
    chosen = member[None] == members
    squares = jnp.stack(
        [
            jnp.sum(jnp.where(chosen, (weight * weight)[None], 0.0), axis=(1, 2)),
            jnp.sum(jnp.where(chosen, (update * update)[None], 0.0), axis=(1, 2)),
        ]
    )
    squares = lax.psum(squares, "shard")
    weight_sizes = jnp.sqrt(squares[0])
    update_sizes = jnp.sqrt(squares[1])
    trust_ratios = weight_sizes / (update_sizes + 1e-06)
    ratio = jnp.where(
        member == 0,
        trust_ratios[0],
        jnp.where(member == 1, trust_ratios[1], jnp.where(member == 2, trust_ratios[2], trust_ratios[3])),
    )
    updated = (weight - 0.01 * ratio * update).astype(jnp.bfloat16)
    gather_rows = padded_width(block_rows, 2 * ROW_TILE)
    updated = jnp.pad(updated, ((0, gather_rows - block_rows), (0, 0)))
    gathered = lax.all_gather(updated, "shard", axis=0, tiled=False)
    full_query, full_output, full_norm, full_bias = unpack(gathered, shapes)
    firsts = unpack(moment_next, shapes)
    seconds = unpack(second_next, shapes)

    def natural(parts, count):
        query, output, norm, bias = parts
        lead = (count,) if count else ()
        return (
            query.reshape(lead + shapes[0]).reshape((-1,) + shapes[0][1:]),
            output.reshape(lead + shapes[1]).reshape((-1,) + shapes[1][1:]),
            norm.reshape(-1),
            bias.reshape(lead + shapes[3]).reshape((-1,) + shapes[3][1:]),
        )

    full = natural((full_query, full_output, full_norm, full_bias), shards)
    firsts = natural(firsts, 0)
    seconds = natural(seconds, 0)
    norm_table = jnp.stack([weight_sizes, update_sizes])
    return (
        full[0],
        full[1],
        full[2],
        full[3],
        firsts[0],
        firsts[1],
        firsts[2],
        firsts[3],
        seconds[0],
        seconds[1],
        seconds[2],
        seconds[3],
        norm_table,
        trust_ratios,
    )


def solution(mesh):
    shards = mesh.shape["shard"]
    replicas = mesh.shape["replica"]
    placed = (
        P(("replica", "shard"), None, None),
        P(("replica", "shard"), None, None),
        P(("replica", "shard"), None),
        P(("replica", "shard"), None, None),
        P("shard", None),
        P("shard", None),
        P("shard"),
        P("shard", None),
        P("shard", None),
        P("shard", None),
        P("shard"),
        P("shard", None),
        P("shard", None),
        P("shard", None),
        P("shard"),
        P("shard", None),
    )

    def body(*args):
        return on_device(*args, shards=shards, replicas=replicas)

    return jax.shard_map(
        body,
        mesh=mesh,
        in_specs=placed,
        out_specs=(
            P(),
            P(),
            P(),
            P(),
            P("shard", None),
            P("shard", None),
            P("shard"),
            P("shard", None),
            P("shard", None),
            P("shard", None),
            P("shard"),
            P("shard", None),
            P(),
            P(),
        ),
        check_vma=False,
    )
```

```python
import jax
import jax.numpy as jnp
from jax import lax
from jax.sharding import PartitionSpec as P

LANES = 128
CORE_BIT = 0
Y_GROUP = (2, 1)
REPLICA_SPLITS = ((0b11 << 3, 4), (1 << 5, 5))
REPLICA_BUTTERFLY = (1 << 3, 1 << 6, 1 << 7, 0b11 << 7)
ROW_TILE = 8
SHARD_BUTTERFLY = (1, 0b01 << 1, 0b11 << 1)
AXES = ("replica", "shard")


def step_math(summed, moment, second, weight, decay_rate):
    moment_next = 0.5 * moment + 0.5 * summed
    second_next = 0.5 * second + 0.5 * summed * summed
    update = moment_next / (jnp.sqrt(second_next) + 1e-06) + decay_rate * weight
    return (moment_next, second_next, update)


def padded_width(width, multiple):
    return -(-width // multiple) * multiple


def bit_of(index, bit):
    return (index >> bit) & 1


def exchange(value, mask, devices):
    return lax.ppermute(value, AXES, [(d, d ^ mask) for d in range(devices)])


def masks_of(group):
    width = len(group)
    return [
        sum(((t >> (width - 1 - j)) & 1) << group[j] for j in range(width))
        for t in range(1 << width)
    ]


def part_of(index, group):
    return sum(bit_of(index, bit) << (len(group) - 1 - j) for j, bit in enumerate(group))


def reduce_blocks(packed, devices):
    index = lax.axis_index(AXES)
    shards = packed.shape[0]
    pairs = packed.reshape((shards // 2, 2) + packed.shape[1:])
    mine = bit_of(index, CORE_BIT)
    keep = lax.dynamic_index_in_dim(pairs, mine, 1, keepdims=False)
    send = lax.dynamic_index_in_dim(pairs, 1 - mine, 1, keepdims=False)
    blocks = keep + exchange(send, 1 << CORE_BIT, devices)
    mine = part_of(index, Y_GROUP)
    masks = masks_of(Y_GROUP)
    total = lax.dynamic_index_in_dim(blocks, mine, 0, keepdims=False)
    for t in range(1, len(masks)):
        part = lax.dynamic_index_in_dim(blocks, mine ^ t, 0, keepdims=False)
        total = total + exchange(part, masks[t], devices)
    rows, lanes = total.shape
    multiple = ROW_TILE << len(REPLICA_SPLITS)
    total = jnp.pad(total, ((0, padded_width(rows, multiple) - rows), (0, 0)))
    for mask, bit in REPLICA_SPLITS:
        halves = total.reshape((2, total.shape[0] // 2, lanes))
        mine = bit_of(index, bit)
        keep = lax.dynamic_index_in_dim(halves, mine, 0, keepdims=False)
        send = lax.dynamic_index_in_dim(halves, 1 - mine, 0, keepdims=False)
        total = keep + exchange(send, mask, devices)
    for mask in REPLICA_BUTTERFLY:
        total = total + exchange(total, mask, devices)
    for mask, bit in reversed(REPLICA_SPLITS):
        other = exchange(total, mask, devices)
        first = bit_of(index, bit) == 0
        total = jnp.concatenate([jnp.where(first, total, other), jnp.where(first, other, total)], axis=0)
    return total[:rows]


def as_tile(value, rows, lanes):
    if value.size == rows * lanes:
        return value.reshape(rows, lanes)
    flat = value.reshape(1, -1)
    flat = jnp.pad(flat, ((0, 0), (0, lanes * (-(-flat.shape[1] // lanes)) - flat.shape[1])))
    flat = flat.reshape(-1, lanes)
    return jnp.pad(flat, ((0, rows - flat.shape[0]), (0, 0)))


def on_device(
    grad_query,
    grad_output,
    grad_norm,
    grad_bias,
    weight_query,
    weight_output,
    weight_norm,
    weight_bias,
    first_query,
    first_output,
    first_norm,
    first_bias,
    second_query,
    second_output,
    second_norm,
    second_bias,
    shards,
    replicas,
):
    weights = (weight_query, weight_output, weight_norm, weight_bias)
    moments = (first_query, first_output, first_norm, first_bias)
    seconds = (second_query, second_output, second_norm, second_bias)
    decay_rates = (0.01, 0.01, 0.0, 0.0)
    gradients = (grad_query[0], grad_output[0], grad_norm[0], grad_bias[0])
    sizes = [weight.size for weight in weights]
    offsets = [sum(sizes[:member]) for member in range(4)]
    total = sum(sizes)
    devices = shards * replicas
    query_rows, lanes = weight_query.shape
    output_rows = weight_output.size // lanes
    small = jnp.concatenate(
        [grad_norm[0].reshape(shards, -1), grad_bias[0].reshape(shards, -1)], axis=1
    )
    small_width = small.shape[1]
    small = jnp.pad(small, ((0, 0), (0, lanes - small_width))).reshape(shards, 1, lanes)
    small = jnp.pad(small, ((0, 0), (0, 7), (0, 0)))
    packed = jnp.concatenate(
        [
            grad_query[0].reshape(shards, query_rows, lanes),
            grad_output[0].reshape(shards, output_rows, lanes),
            small,
        ],
        axis=1,
    )
    block = reduce_blocks(packed, devices)
    summed_rest = block[query_rows + output_rows, :small_width]
    summed_all = [
        block[:query_rows],
        block[query_rows : query_rows + output_rows].reshape(weight_output.shape),
        summed_rest[: weight_norm.size].reshape(weight_norm.shape),
        summed_rest[weight_norm.size :].reshape(weight_bias.shape),
    ]
    results = [
        step_math(
            summed_all[member],
            moments[member],
            seconds[member],
            weights[member],
            decay_rates[member],
        )
        for member in range(4)
    ]
    terms = [as_tile(weight, query_rows, lanes) for weight in weights]
    terms += [as_tile(result[2], query_rows, lanes) for result in results]
    stacked = jnp.stack(terms)
    squares = jnp.sum(stacked * stacked, axis=(1, 2))
    for mask in SHARD_BUTTERFLY:
        squares = squares + exchange(squares, mask, shards * replicas)
    weight_sizes = jnp.sqrt(squares[:4])
    update_sizes = jnp.sqrt(squares[4:])
    trust_ratios = weight_sizes / (update_sizes + 1e-06)
    shards_out = [
        (weights[member] - 0.01 * trust_ratios[member] * results[member][2]).astype(jnp.bfloat16).reshape(-1)
        for member in range(4)
    ]
    out_width = padded_width(total, LANES)
    shards_out.append(jnp.zeros((out_width - total,), jnp.bfloat16))
    gathered = lax.all_gather(jnp.concatenate(shards_out), "shard", axis=0, tiled=False)
    full = [
        gathered[:, offsets[member] : offsets[member] + sizes[member]].reshape(
            (shards * weights[member].shape[0],) + weights[member].shape[1:]
        )
        for member in range(4)
    ]
    norm_table = jnp.stack([weight_sizes, update_sizes])
    return (
        full[0],
        full[1],
        full[2],
        full[3],
        results[0][0],
        results[1][0],
        results[2][0],
        results[3][0],
        results[0][1],
        results[1][1],
        results[2][1],
        results[3][1],
        norm_table,
        trust_ratios,
    )


def solution(mesh):
    shards = mesh.shape["shard"]
    replicas = mesh.shape["replica"]
    placed = (
        P(("replica", "shard"), None, None),
        P(("replica", "shard"), None, None),
        P(("replica", "shard"), None),
        P(("replica", "shard"), None, None),
        P("shard", None),
        P("shard", None),
        P("shard"),
        P("shard", None),
        P("shard", None),
        P("shard", None),
        P("shard"),
        P("shard", None),
        P("shard", None),
        P("shard", None),
        P("shard"),
        P("shard", None),
    )

    def body(*args):
        return on_device(*args, shards=shards, replicas=replicas)

    return jax.shard_map(
        body,
        mesh=mesh,
        in_specs=placed,
        out_specs=(
            P(),
            P(),
            P(),
            P(),
            P("shard", None),
            P("shard", None),
            P("shard"),
            P("shard", None),
            P("shard", None),
            P("shard", None),
            P("shard"),
            P("shard", None),
            P(),
            P(),
        ),
        check_vma=False,
    )
```

```python
import jax
import jax.numpy as jnp
from jax import lax
from jax.sharding import PartitionSpec as P

LANES = 128
CORE_BIT = 0
Y_GROUP = (2, 1)
REPLICA_SPLITS = ((0b11 << 3, 4), (1 << 5, 5), (1 << 3, 3))
REPLICA_BUTTERFLY = (1 << 6, 1 << 7, 0b11 << 7)
ROW_TILE = 8
AXES = ("replica", "shard")


def step_math(summed, moment, second, weight, decay_rate):
    moment_next = 0.5 * moment + 0.5 * summed
    second_next = 0.5 * second + 0.5 * summed * summed
    update = moment_next / (jnp.sqrt(second_next) + 1e-06) + decay_rate * weight
    return (moment_next, second_next, update)


def padded_width(width, multiple):
    return -(-width // multiple) * multiple


def bit_of(index, bit):
    return (index >> bit) & 1


def exchange(value, mask, devices):
    return lax.ppermute(value, AXES, [(d, d ^ mask) for d in range(devices)])


def masks_of(group):
    width = len(group)
    return [
        sum(((t >> (width - 1 - j)) & 1) << group[j] for j in range(width))
        for t in range(1 << width)
    ]


def part_of(index, group):
    return sum(bit_of(index, bit) << (len(group) - 1 - j) for j, bit in enumerate(group))


def reduce_blocks(packed, devices):
    index = lax.axis_index(AXES)
    shards = packed.shape[0]
    pairs = packed.reshape((shards // 2, 2) + packed.shape[1:])
    mine = bit_of(index, CORE_BIT)
    keep = lax.dynamic_index_in_dim(pairs, mine, 1, keepdims=False)
    send = lax.dynamic_index_in_dim(pairs, 1 - mine, 1, keepdims=False)
    blocks = keep + exchange(send, 1 << CORE_BIT, devices)
    mine = part_of(index, Y_GROUP)
    masks = masks_of(Y_GROUP)
    total = lax.dynamic_index_in_dim(blocks, mine, 0, keepdims=False)
    for t in range(1, len(masks)):
        part = lax.dynamic_index_in_dim(blocks, mine ^ t, 0, keepdims=False)
        total = total + exchange(part, masks[t], devices)
    rows, lanes = total.shape
    multiple = ROW_TILE << (len(REPLICA_SPLITS) - 1)
    total = jnp.pad(total, ((0, padded_width(rows, multiple) - rows), (0, 0)))
    for mask, bit in REPLICA_SPLITS:
        halves = total.reshape((2, total.shape[0] // 2, lanes))
        mine = bit_of(index, bit)
        keep = lax.dynamic_index_in_dim(halves, mine, 0, keepdims=False)
        send = lax.dynamic_index_in_dim(halves, 1 - mine, 0, keepdims=False)
        total = keep + exchange(send, mask, devices)
    for mask in REPLICA_BUTTERFLY:
        total = total + exchange(total, mask, devices)
    for mask, bit in reversed(REPLICA_SPLITS):
        other = exchange(total, mask, devices)
        first = bit_of(index, bit) == 0
        total = jnp.concatenate([jnp.where(first, total, other), jnp.where(first, other, total)], axis=0)
    return total[:rows]


def as_tile(value, rows, lanes):
    if value.size == rows * lanes:
        return value.reshape(rows, lanes)
    flat = value.reshape(1, -1)
    flat = jnp.pad(flat, ((0, 0), (0, lanes * (-(-flat.shape[1] // lanes)) - flat.shape[1])))
    flat = flat.reshape(-1, lanes)
    return jnp.pad(flat, ((0, rows - flat.shape[0]), (0, 0)))


def on_device(
    grad_query,
    grad_output,
    grad_norm,
    grad_bias,
    weight_query,
    weight_output,
    weight_norm,
    weight_bias,
    first_query,
    first_output,
    first_norm,
    first_bias,
    second_query,
    second_output,
    second_norm,
    second_bias,
    shards,
    replicas,
):
    weights = (weight_query, weight_output, weight_norm, weight_bias)
    moments = (first_query, first_output, first_norm, first_bias)
    seconds = (second_query, second_output, second_norm, second_bias)
    decay_rates = (0.01, 0.01, 0.0, 0.0)
    gradients = (grad_query[0], grad_output[0], grad_norm[0], grad_bias[0])
    sizes = [weight.size for weight in weights]
    offsets = [sum(sizes[:member]) for member in range(4)]
    total = sum(sizes)
    devices = shards * replicas
    query_rows, lanes = weight_query.shape
    output_rows = weight_output.size // lanes
    small = jnp.concatenate(
        [grad_norm[0].reshape(shards, -1), grad_bias[0].reshape(shards, -1)], axis=1
    )
    small_width = small.shape[1]
    small = jnp.pad(small, ((0, 0), (0, lanes - small_width))).reshape(shards, 1, lanes)
    small = jnp.pad(small, ((0, 0), (0, 7), (0, 0)))
    packed = jnp.concatenate(
        [
            grad_query[0].reshape(shards, query_rows, lanes),
            grad_output[0].reshape(shards, output_rows, lanes),
            small,
        ],
        axis=1,
    )
    block = reduce_blocks(packed, devices)
    summed_rest = block[query_rows + output_rows, :small_width]
    summed_all = [
        block[:query_rows],
        block[query_rows : query_rows + output_rows].reshape(weight_output.shape),
        summed_rest[: weight_norm.size].reshape(weight_norm.shape),
        summed_rest[weight_norm.size :].reshape(weight_bias.shape),
    ]
    results = [
        step_math(
            summed_all[member],
            moments[member],
            seconds[member],
            weights[member],
            decay_rates[member],
        )
        for member in range(4)
    ]
    terms = [as_tile(weight, query_rows, lanes) for weight in weights]
    terms += [as_tile(result[2], query_rows, lanes) for result in results]
    stacked = jnp.stack(terms)
    squares = lax.psum(jnp.sum(stacked * stacked, axis=(1, 2)), "shard")
    weight_sizes = jnp.sqrt(squares[:4])
    update_sizes = jnp.sqrt(squares[4:])
    trust_ratios = weight_sizes / (update_sizes + 1e-06)
    shards_out = [
        (weights[member] - 0.01 * trust_ratios[member] * results[member][2]).astype(jnp.bfloat16).reshape(-1)
        for member in range(4)
    ]
    out_width = padded_width(total, LANES)
    shards_out.append(jnp.zeros((out_width - total,), jnp.bfloat16))
    gathered = lax.all_gather(jnp.concatenate(shards_out), "shard", axis=0, tiled=False)
    full = [
        gathered[:, offsets[member] : offsets[member] + sizes[member]].reshape(
            (shards * weights[member].shape[0],) + weights[member].shape[1:]
        )
        for member in range(4)
    ]
    norm_table = jnp.stack([weight_sizes, update_sizes])
    return (
        full[0],
        full[1],
        full[2],
        full[3],
        results[0][0],
        results[1][0],
        results[2][0],
        results[3][0],
        results[0][1],
        results[1][1],
        results[2][1],
        results[3][1],
        norm_table,
        trust_ratios,
    )


def solution(mesh):
    shards = mesh.shape["shard"]
    replicas = mesh.shape["replica"]
    placed = (
        P(("replica", "shard"), None, None),
        P(("replica", "shard"), None, None),
        P(("replica", "shard"), None),
        P(("replica", "shard"), None, None),
        P("shard", None),
        P("shard", None),
        P("shard"),
        P("shard", None),
        P("shard", None),
        P("shard", None),
        P("shard"),
        P("shard", None),
        P("shard", None),
        P("shard", None),
        P("shard"),
        P("shard", None),
    )

    def body(*args):
        return on_device(*args, shards=shards, replicas=replicas)

    return jax.shard_map(
        body,
        mesh=mesh,
        in_specs=placed,
        out_specs=(
            P(),
            P(),
            P(),
            P(),
            P("shard", None),
            P("shard", None),
            P("shard"),
            P("shard", None),
            P("shard", None),
            P("shard", None),
            P("shard"),
            P("shard", None),
            P(),
            P(),
        ),
        check_vma=False,
    )
```

```python
import jax
import jax.numpy as jnp
from jax import lax
from jax.sharding import PartitionSpec as P

LANES = 128
CORE_BIT = 0
Y_GROUP = (2, 1)
REPLICA_SPLITS = ((0b11 << 3, 4), (1 << 5, 5))
REPLICA_BUTTERFLY = (1 << 3, 1 << 6, 1 << 7, 0b11 << 7)
ROW_TILE = 8
AXES = ("replica", "shard")


def step_math(summed, moment, second, weight, decay_rate):
    moment_next = 0.5 * moment + 0.5 * summed
    second_next = 0.5 * second + 0.5 * summed * summed
    update = moment_next / (jnp.sqrt(second_next) + 1e-06) + decay_rate * weight
    return (moment_next, second_next, update)


def padded_width(width, multiple):
    return -(-width // multiple) * multiple


def bit_of(index, bit):
    return (index >> bit) & 1


def exchange(value, mask, devices):
    return lax.ppermute(value, AXES, [(d, d ^ mask) for d in range(devices)])


def masks_of(group):
    width = len(group)
    return [
        sum(((t >> (width - 1 - j)) & 1) << group[j] for j in range(width))
        for t in range(1 << width)
    ]


def part_of(index, group):
    return sum(bit_of(index, bit) << (len(group) - 1 - j) for j, bit in enumerate(group))


def reduce_blocks(packed, devices):
    index = lax.axis_index(AXES)
    shards = packed.shape[0]
    pairs = packed.reshape((shards // 2, 2) + packed.shape[1:])
    mine = bit_of(index, CORE_BIT)
    keep = lax.dynamic_index_in_dim(pairs, mine, 1, keepdims=False)
    send = lax.dynamic_index_in_dim(pairs, 1 - mine, 1, keepdims=False)
    blocks = keep + exchange(send, 1 << CORE_BIT, devices)
    mine = part_of(index, Y_GROUP)
    masks = masks_of(Y_GROUP)
    total = lax.dynamic_index_in_dim(blocks, mine, 0, keepdims=False)
    for t in range(1, len(masks)):
        part = lax.dynamic_index_in_dim(blocks, mine ^ t, 0, keepdims=False)
        total = total + exchange(part, masks[t], devices)
    rows, lanes = total.shape
    multiple = ROW_TILE << len(REPLICA_SPLITS)
    total = jnp.pad(total, ((0, padded_width(rows, multiple) - rows), (0, 0)))
    for mask, bit in REPLICA_SPLITS:
        halves = total.reshape((2, total.shape[0] // 2, lanes))
        mine = bit_of(index, bit)
        keep = lax.dynamic_index_in_dim(halves, mine, 0, keepdims=False)
        send = lax.dynamic_index_in_dim(halves, 1 - mine, 0, keepdims=False)
        total = keep + exchange(send, mask, devices)
    for mask in REPLICA_BUTTERFLY:
        total = total + exchange(total, mask, devices)
    for mask, bit in reversed(REPLICA_SPLITS):
        other = exchange(total, mask, devices)
        first = bit_of(index, bit) == 0
        total = jnp.concatenate([jnp.where(first, total, other), jnp.where(first, other, total)], axis=0)
    return total[:rows]


def as_tile(value, rows, lanes):
    if value.size == rows * lanes:
        return value.reshape(rows, lanes)
    flat = value.reshape(1, -1)
    flat = jnp.pad(flat, ((0, 0), (0, lanes * (-(-flat.shape[1] // lanes)) - flat.shape[1])))
    flat = flat.reshape(-1, lanes)
    return jnp.pad(flat, ((0, rows - flat.shape[0]), (0, 0)))


def on_device(
    grad_query,
    grad_output,
    grad_norm,
    grad_bias,
    weight_query,
    weight_output,
    weight_norm,
    weight_bias,
    first_query,
    first_output,
    first_norm,
    first_bias,
    second_query,
    second_output,
    second_norm,
    second_bias,
    shards,
    replicas,
):
    weights = (weight_query, weight_output, weight_norm, weight_bias)
    moments = (first_query, first_output, first_norm, first_bias)
    seconds = (second_query, second_output, second_norm, second_bias)
    decay_rates = (0.01, 0.01, 0.0, 0.0)
    gradients = (grad_query[0], grad_output[0], grad_norm[0], grad_bias[0])
    sizes = [weight.size for weight in weights]
    offsets = [sum(sizes[:member]) for member in range(4)]
    total = sum(sizes)
    devices = shards * replicas
    query_rows, lanes = weight_query.shape
    output_rows = weight_output.size // lanes
    small = jnp.concatenate(
        [grad_norm[0].reshape(shards, -1), grad_bias[0].reshape(shards, -1)], axis=1
    )
    small_width = small.shape[1]
    small = jnp.pad(small, ((0, 0), (0, lanes - small_width))).reshape(shards, 1, lanes)
    small = jnp.pad(small, ((0, 0), (0, 7), (0, 0)))
    packed = jnp.concatenate(
        [
            grad_query[0].reshape(shards, query_rows, lanes),
            grad_output[0].reshape(shards, output_rows, lanes),
            small,
        ],
        axis=1,
    )
    block = reduce_blocks(packed, devices)
    summed_rest = block[query_rows + output_rows, :small_width]
    summed_all = [
        block[:query_rows],
        block[query_rows : query_rows + output_rows].reshape(weight_output.shape),
        summed_rest[: weight_norm.size].reshape(weight_norm.shape),
        summed_rest[weight_norm.size :].reshape(weight_bias.shape),
    ]
    results = [
        step_math(
            summed_all[member],
            moments[member],
            seconds[member],
            weights[member],
            decay_rates[member],
        )
        for member in range(4)
    ]
    terms = [as_tile(weight, query_rows, lanes) for weight in weights]
    terms += [as_tile(result[2], query_rows, lanes) for result in results]
    stacked = jnp.stack(terms)
    squares = lax.psum(jnp.sum(stacked * stacked, axis=(1, 2)), "shard")
    weight_sizes = jnp.sqrt(squares[:4])
    update_sizes = jnp.sqrt(squares[4:])
    trust_ratios = weight_sizes / (update_sizes + 1e-06)
    updated = [
        (weights[member] - 0.01 * trust_ratios[member] * results[member][2]).astype(jnp.bfloat16)
        for member in range(4)
    ]
    rest = jnp.concatenate([updated[2].reshape(-1), updated[3].reshape(-1)])
    rest = jnp.pad(rest, (0, lanes - rest.shape[0])).reshape(1, lanes)
    payload = jnp.concatenate([updated[0], updated[1].reshape(-1, lanes), rest], axis=0)
    gather_rows = padded_width(payload.shape[0], 2 * ROW_TILE)
    payload = jnp.pad(payload, ((0, gather_rows - payload.shape[0]), (0, 0)))
    gathered = lax.all_gather(payload, "shard", axis=0, tiled=False)
    gathered_rest = gathered[:, query_rows + output_rows]
    norm_size = weight_norm.size
    full = [
        gathered[:, :query_rows].reshape(-1, lanes),
        gathered[:, query_rows : query_rows + output_rows]
        .reshape((shards,) + weight_output.shape)
        .reshape((-1,) + weight_output.shape[1:]),
        gathered_rest[:, :norm_size].reshape(-1),
        gathered_rest[:, norm_size : norm_size + weight_bias.size]
        .reshape((shards,) + weight_bias.shape)
        .reshape((-1,) + weight_bias.shape[1:]),
    ]
    norm_table = jnp.stack([weight_sizes, update_sizes])
    return (
        full[0],
        full[1],
        full[2],
        full[3],
        results[0][0],
        results[1][0],
        results[2][0],
        results[3][0],
        results[0][1],
        results[1][1],
        results[2][1],
        results[3][1],
        norm_table,
        trust_ratios,
    )


def solution(mesh):
    shards = mesh.shape["shard"]
    replicas = mesh.shape["replica"]
    placed = (
        P(("replica", "shard"), None, None),
        P(("replica", "shard"), None, None),
        P(("replica", "shard"), None),
        P(("replica", "shard"), None, None),
        P("shard", None),
        P("shard", None),
        P("shard"),
        P("shard", None),
        P("shard", None),
        P("shard", None),
        P("shard"),
        P("shard", None),
        P("shard", None),
        P("shard", None),
        P("shard"),
        P("shard", None),
    )

    def body(*args):
        return on_device(*args, shards=shards, replicas=replicas)

    return jax.shard_map(
        body,
        mesh=mesh,
        in_specs=placed,
        out_specs=(
            P(),
            P(),
            P(),
            P(),
            P("shard", None),
            P("shard", None),
            P("shard"),
            P("shard", None),
            P("shard", None),
            P("shard", None),
            P("shard"),
            P("shard", None),
            P(),
            P(),
        ),
        check_vma=False,
    )
```

```python
import jax
import jax.numpy as jnp
from jax import lax
from jax.sharding import PartitionSpec as P

LANES = 128
CORE_BIT = 0
Y_GROUP = (2, 1)
REPLICA_SPLITS = ((0b11 << 3, 4), (1 << 5, 5))
REPLICA_BUTTERFLY = (1 << 3, 1 << 6, 1 << 7, 0b11 << 7)
ROW_TILE = 8
AXES = ("replica", "shard")


def step_math(summed, moment, second, weight, decay_rate):
    moment_next = 0.5 * moment + 0.5 * summed
    second_next = 0.5 * second + 0.5 * summed * summed
    update = moment_next / (jnp.sqrt(second_next) + 1e-06) + decay_rate * weight
    return (moment_next, second_next, update)


def padded_width(width, multiple):
    return -(-width // multiple) * multiple


def bit_of(index, bit):
    return (index >> bit) & 1


def exchange(value, mask, devices):
    return lax.ppermute(value, AXES, [(d, d ^ mask) for d in range(devices)])


def masks_of(group):
    width = len(group)
    return [
        sum(((t >> (width - 1 - j)) & 1) << group[j] for j in range(width))
        for t in range(1 << width)
    ]


def part_of(index, group):
    return sum(bit_of(index, bit) << (len(group) - 1 - j) for j, bit in enumerate(group))


def reduce_blocks(packed, devices):
    index = lax.axis_index(AXES)
    shards = packed.shape[0]
    pairs = packed.reshape((shards // 2, 2) + packed.shape[1:])
    mine = bit_of(index, CORE_BIT)
    keep = lax.dynamic_index_in_dim(pairs, mine, 1, keepdims=False)
    send = lax.dynamic_index_in_dim(pairs, 1 - mine, 1, keepdims=False)
    blocks = keep + exchange(send, 1 << CORE_BIT, devices)
    mine = part_of(index, Y_GROUP)
    masks = masks_of(Y_GROUP)
    total = lax.dynamic_index_in_dim(blocks, mine, 0, keepdims=False)
    for t in range(1, len(masks)):
        part = lax.dynamic_index_in_dim(blocks, mine ^ t, 0, keepdims=False)
        total = total + exchange(part, masks[t], devices)
    rows, lanes = total.shape
    multiple = ROW_TILE << len(REPLICA_SPLITS)
    total = jnp.pad(total, ((0, padded_width(rows, multiple) - rows), (0, 0)))
    for mask, bit in REPLICA_SPLITS:
        halves = total.reshape((2, total.shape[0] // 2, lanes))
        mine = bit_of(index, bit)
        keep = lax.dynamic_index_in_dim(halves, mine, 0, keepdims=False)
        send = lax.dynamic_index_in_dim(halves, 1 - mine, 0, keepdims=False)
        total = keep + exchange(send, mask, devices)
    for mask in REPLICA_BUTTERFLY:
        total = total + exchange(total, mask, devices)
    for mask, bit in reversed(REPLICA_SPLITS):
        other = exchange(total, mask, devices)
        first = bit_of(index, bit) == 0
        total = jnp.concatenate([jnp.where(first, total, other), jnp.where(first, other, total)], axis=0)
    return total[:rows]


def as_tile(value, rows, lanes):
    if value.size == rows * lanes:
        return value.reshape(rows, lanes)
    flat = value.reshape(1, -1)
    flat = jnp.pad(flat, ((0, 0), (0, lanes * (-(-flat.shape[1] // lanes)) - flat.shape[1])))
    flat = flat.reshape(-1, lanes)
    return jnp.pad(flat, ((0, rows - flat.shape[0]), (0, 0)))


def on_device(
    grad_query,
    grad_output,
    grad_norm,
    grad_bias,
    weight_query,
    weight_output,
    weight_norm,
    weight_bias,
    first_query,
    first_output,
    first_norm,
    first_bias,
    second_query,
    second_output,
    second_norm,
    second_bias,
    shards,
    replicas,
):
    weights = (weight_query, weight_output, weight_norm, weight_bias)
    moments = (first_query, first_output, first_norm, first_bias)
    seconds = (second_query, second_output, second_norm, second_bias)
    decay_rates = (0.01, 0.01, 0.0, 0.0)
    gradients = (grad_query[0], grad_output[0], grad_norm[0], grad_bias[0])
    sizes = [weight.size for weight in weights]
    offsets = [sum(sizes[:member]) for member in range(4)]
    total = sum(sizes)
    devices = shards * replicas
    query_rows, lanes = weight_query.shape
    output_rows = weight_output.size // lanes
    small = jnp.concatenate(
        [grad_norm[0].reshape(shards, -1), grad_bias[0].reshape(shards, -1)], axis=1
    )
    small_width = small.shape[1]
    small = jnp.pad(small, ((0, 0), (0, lanes - small_width))).reshape(shards, 1, lanes)
    small = jnp.pad(small, ((0, 0), (0, 7), (0, 0)))
    packed = jnp.concatenate(
        [
            grad_query[0].reshape(shards, query_rows, lanes),
            grad_output[0].reshape(shards, output_rows, lanes),
            small,
        ],
        axis=1,
    )
    block = reduce_blocks(packed, devices)
    summed_rest = block[query_rows + output_rows, :small_width]
    summed_all = [
        block[:query_rows],
        block[query_rows : query_rows + output_rows].reshape(weight_output.shape),
        summed_rest[: weight_norm.size].reshape(weight_norm.shape),
        summed_rest[weight_norm.size :].reshape(weight_bias.shape),
    ]
    results = [
        step_math(
            summed_all[member],
            moments[member],
            seconds[member],
            weights[member],
            decay_rates[member],
        )
        for member in range(4)
    ]
    terms = [as_tile(weight, query_rows, lanes) for weight in weights]
    terms += [as_tile(result[2], query_rows, lanes) for result in results]
    stacked = jnp.stack(terms)
    squares = lax.psum(jnp.sum(stacked * stacked, axis=(1, 2)), "shard")
    weight_sizes = jnp.sqrt(squares[:4])
    update_sizes = jnp.sqrt(squares[4:])
    trust_ratios = weight_sizes / (update_sizes + 1e-06)
    members = len(weights)
    ratios = (0.01 * trust_ratios).reshape(members, 1, 1)
    updated = (stacked[:members] - ratios * stacked[members:]).astype(jnp.bfloat16)
    norm_size = weight_norm.size
    rest = jnp.concatenate([updated[2, 0, :norm_size], updated[3, 0, : weight_bias.size]])
    rest = jnp.pad(rest, (0, lanes - rest.shape[0])).reshape(1, lanes)
    payload = jnp.concatenate([updated[0], updated[1], rest], axis=0)
    gather_rows = padded_width(payload.shape[0], 2 * ROW_TILE)
    payload = jnp.pad(payload, ((0, gather_rows - payload.shape[0]), (0, 0)))
    gathered = lax.all_gather(payload, "shard", axis=0, tiled=False)
    gathered_rest = gathered[:, query_rows + output_rows]
    full = [
        gathered[:, :query_rows].reshape(-1, lanes),
        gathered[:, query_rows : query_rows + output_rows]
        .reshape((shards,) + weight_output.shape)
        .reshape((-1,) + weight_output.shape[1:]),
        gathered_rest[:, :norm_size].reshape(-1),
        gathered_rest[:, norm_size : norm_size + weight_bias.size]
        .reshape((shards,) + weight_bias.shape)
        .reshape((-1,) + weight_bias.shape[1:]),
    ]
    norm_table = jnp.stack([weight_sizes, update_sizes])
    return (
        full[0],
        full[1],
        full[2],
        full[3],
        results[0][0],
        results[1][0],
        results[2][0],
        results[3][0],
        results[0][1],
        results[1][1],
        results[2][1],
        results[3][1],
        norm_table,
        trust_ratios,
    )


def solution(mesh):
    shards = mesh.shape["shard"]
    replicas = mesh.shape["replica"]
    placed = (
        P(("replica", "shard"), None, None),
        P(("replica", "shard"), None, None),
        P(("replica", "shard"), None),
        P(("replica", "shard"), None, None),
        P("shard", None),
        P("shard", None),
        P("shard"),
        P("shard", None),
        P("shard", None),
        P("shard", None),
        P("shard"),
        P("shard", None),
        P("shard", None),
        P("shard", None),
        P("shard"),
        P("shard", None),
    )

    def body(*args):
        return on_device(*args, shards=shards, replicas=replicas)

    return jax.shard_map(
        body,
        mesh=mesh,
        in_specs=placed,
        out_specs=(
            P(),
            P(),
            P(),
            P(),
            P("shard", None),
            P("shard", None),
            P("shard"),
            P("shard", None),
            P("shard", None),
            P("shard", None),
            P("shard"),
            P("shard", None),
            P(),
            P(),
        ),
        check_vma=False,
    )
```

```python
import jax
import jax.numpy as jnp
from jax import lax
from jax.sharding import PartitionSpec as P

LANES = 128
CORE_BIT = 0
Y_GROUP = (2, 1)
REPLICA_SPLITS = ((0b11 << 3, 4), (1 << 5, 5))
REPLICA_BUTTERFLY = (1 << 3, 1 << 6, 1 << 7, 0b11 << 7)
ROW_TILE = 8
AXES = ("replica", "shard")


def step_math(summed, moment, second, weight, decay_rate):
    moment_next = 0.5 * moment + 0.5 * summed
    second_next = 0.5 * second + 0.5 * summed * summed
    update = moment_next / (jnp.sqrt(second_next) + 1e-06) + decay_rate * weight
    return (moment_next, second_next, update)


def padded_width(width, multiple):
    return -(-width // multiple) * multiple


def bit_of(index, bit):
    return (index >> bit) & 1


def exchange(value, mask, devices):
    return lax.ppermute(value, AXES, [(d, d ^ mask) for d in range(devices)])


def masks_of(group):
    width = len(group)
    return [
        sum(((t >> (width - 1 - j)) & 1) << group[j] for j in range(width))
        for t in range(1 << width)
    ]


def part_of(index, group):
    return sum(bit_of(index, bit) << (len(group) - 1 - j) for j, bit in enumerate(group))


def reduce_blocks(packed, devices):
    index = lax.axis_index(AXES)
    shards = packed.shape[0]
    pairs = packed.reshape((shards // 2, 2) + packed.shape[1:])
    mine = bit_of(index, CORE_BIT)
    keep = lax.dynamic_index_in_dim(pairs, mine, 1, keepdims=False)
    send = lax.dynamic_index_in_dim(pairs, 1 - mine, 1, keepdims=False)
    blocks = keep + exchange(send, 1 << CORE_BIT, devices)
    mine = part_of(index, Y_GROUP)
    masks = masks_of(Y_GROUP)
    total = lax.dynamic_index_in_dim(blocks, mine, 0, keepdims=False)
    for t in range(1, len(masks)):
        part = lax.dynamic_index_in_dim(blocks, mine ^ t, 0, keepdims=False)
        total = total + exchange(part, masks[t], devices)
    rows, lanes = total.shape
    multiple = ROW_TILE << len(REPLICA_SPLITS)
    total = jnp.pad(total, ((0, padded_width(rows, multiple) - rows), (0, 0)))
    for mask, bit in REPLICA_SPLITS:
        halves = total.reshape((2, total.shape[0] // 2, lanes))
        mine = bit_of(index, bit)
        keep = lax.dynamic_index_in_dim(halves, mine, 0, keepdims=False)
        send = lax.dynamic_index_in_dim(halves, 1 - mine, 0, keepdims=False)
        total = keep + exchange(send, mask, devices)
    for mask in REPLICA_BUTTERFLY:
        total = total + exchange(total, mask, devices)
    for mask, bit in reversed(REPLICA_SPLITS):
        other = exchange(total, mask, devices)
        first = bit_of(index, bit) == 0
        total = jnp.concatenate([jnp.where(first, total, other), jnp.where(first, other, total)], axis=0)
    return total[:rows]


def as_tile(value, rows, lanes):
    if value.size == rows * lanes:
        return value.reshape(rows, lanes)
    flat = value.reshape(1, -1)
    flat = jnp.pad(flat, ((0, 0), (0, lanes * (-(-flat.shape[1] // lanes)) - flat.shape[1])))
    flat = flat.reshape(-1, lanes)
    return jnp.pad(flat, ((0, rows - flat.shape[0]), (0, 0)))


def on_device(
    grad_query,
    grad_output,
    grad_norm,
    grad_bias,
    weight_query,
    weight_output,
    weight_norm,
    weight_bias,
    first_query,
    first_output,
    first_norm,
    first_bias,
    second_query,
    second_output,
    second_norm,
    second_bias,
    shards,
    replicas,
):
    weights = (weight_query, weight_output, weight_norm, weight_bias)
    moments = (first_query, first_output, first_norm, first_bias)
    seconds = (second_query, second_output, second_norm, second_bias)
    decay_rates = (0.01, 0.01, 0.0, 0.0)
    gradients = (grad_query[0], grad_output[0], grad_norm[0], grad_bias[0])
    sizes = [weight.size for weight in weights]
    offsets = [sum(sizes[:member]) for member in range(4)]
    total = sum(sizes)
    devices = shards * replicas
    query_rows, lanes = weight_query.shape
    output_rows = weight_output.size // lanes
    small = jnp.concatenate(
        [grad_norm[0].reshape(shards, -1), grad_bias[0].reshape(shards, -1)], axis=1
    )
    small_width = small.shape[1]
    small = jnp.pad(small, ((0, 0), (0, lanes - small_width))).reshape(shards, 1, lanes)
    small = jnp.pad(small, ((0, 0), (0, 7), (0, 0)))
    packed = jnp.concatenate(
        [
            grad_query[0].reshape(shards, query_rows, lanes),
            grad_output[0].reshape(shards, output_rows, lanes),
            small,
        ],
        axis=1,
    )
    block = reduce_blocks(packed, devices)
    summed_rest = block[query_rows + output_rows, :small_width]
    summed_tiles = [
        block[:query_rows],
        block[query_rows : query_rows + output_rows],
        as_tile(summed_rest[: weight_norm.size], query_rows, lanes),
        as_tile(summed_rest[weight_norm.size :], query_rows, lanes),
    ]
    members = len(weights)
    weight_tiles = jnp.stack([as_tile(weight, query_rows, lanes) for weight in weights])
    decay = jnp.array(decay_rates, jnp.float32).reshape(members, 1, 1)
    moment_tiles, second_tiles, update_tiles = step_math(
        jnp.stack(summed_tiles),
        jnp.stack([as_tile(moment, query_rows, lanes) for moment in moments]),
        jnp.stack([as_tile(second, query_rows, lanes) for second in seconds]),
        weight_tiles,
        decay,
    )

    def untile(tiles):
        return (
            tiles[0],
            tiles[1].reshape(weight_output.shape),
            tiles[2, 0, : weight_norm.size],
            tiles[3, 0, : weight_bias.size].reshape(weight_bias.shape),
        )

    results = list(zip(untile(moment_tiles), untile(second_tiles)))
    stacked = jnp.concatenate([weight_tiles, update_tiles])
    squares = lax.psum(jnp.sum(stacked * stacked, axis=(1, 2)), "shard")
    weight_sizes = jnp.sqrt(squares[:4])
    update_sizes = jnp.sqrt(squares[4:])
    trust_ratios = weight_sizes / (update_sizes + 1e-06)
    members = len(weights)
    ratios = (0.01 * trust_ratios).reshape(members, 1, 1)
    updated = (stacked[:members] - ratios * stacked[members:]).astype(jnp.bfloat16)
    norm_size = weight_norm.size
    rest = jnp.concatenate([updated[2, 0, :norm_size], updated[3, 0, : weight_bias.size]])
    rest = jnp.pad(rest, (0, lanes - rest.shape[0])).reshape(1, lanes)
    payload = jnp.concatenate([updated[0], updated[1], rest], axis=0)
    gather_rows = padded_width(payload.shape[0], 2 * ROW_TILE)
    payload = jnp.pad(payload, ((0, gather_rows - payload.shape[0]), (0, 0)))
    gathered = lax.all_gather(payload, "shard", axis=0, tiled=False)
    gathered_rest = gathered[:, query_rows + output_rows]
    full = [
        gathered[:, :query_rows].reshape(-1, lanes),
        gathered[:, query_rows : query_rows + output_rows]
        .reshape((shards,) + weight_output.shape)
        .reshape((-1,) + weight_output.shape[1:]),
        gathered_rest[:, :norm_size].reshape(-1),
        gathered_rest[:, norm_size : norm_size + weight_bias.size]
        .reshape((shards,) + weight_bias.shape)
        .reshape((-1,) + weight_bias.shape[1:]),
    ]
    norm_table = jnp.stack([weight_sizes, update_sizes])
    return (
        full[0],
        full[1],
        full[2],
        full[3],
        results[0][0],
        results[1][0],
        results[2][0],
        results[3][0],
        results[0][1],
        results[1][1],
        results[2][1],
        results[3][1],
        norm_table,
        trust_ratios,
    )


def solution(mesh):
    shards = mesh.shape["shard"]
    replicas = mesh.shape["replica"]
    placed = (
        P(("replica", "shard"), None, None),
        P(("replica", "shard"), None, None),
        P(("replica", "shard"), None),
        P(("replica", "shard"), None, None),
        P("shard", None),
        P("shard", None),
        P("shard"),
        P("shard", None),
        P("shard", None),
        P("shard", None),
        P("shard"),
        P("shard", None),
        P("shard", None),
        P("shard", None),
        P("shard"),
        P("shard", None),
    )

    def body(*args):
        return on_device(*args, shards=shards, replicas=replicas)

    return jax.shard_map(
        body,
        mesh=mesh,
        in_specs=placed,
        out_specs=(
            P(),
            P(),
            P(),
            P(),
            P("shard", None),
            P("shard", None),
            P("shard"),
            P("shard", None),
            P("shard", None),
            P("shard", None),
            P("shard"),
            P("shard", None),
            P(),
            P(),
        ),
        check_vma=False,
    )
```

```python
import jax
import jax.numpy as jnp
from jax import lax
from jax.sharding import PartitionSpec as P

LANES = 128
CORE_BIT = 0
Y_GROUP = (2, 1)
REPLICA_SPLITS = ((0b11 << 3, 4), (1 << 5, 5))
REPLICA_BUTTERFLY = (1 << 3, 1 << 6, 1 << 7, 0b11 << 7)
ROW_TILE = 8
AXES = ("replica", "shard")


def step_math(summed, moment, second, weight, decay_rate):
    moment_next = 0.5 * moment + 0.5 * summed
    second_next = 0.5 * second + 0.5 * summed * summed
    update = moment_next / (jnp.sqrt(second_next) + 1e-06) + decay_rate * weight
    return (moment_next, second_next, update)


def padded_width(width, multiple):
    return -(-width // multiple) * multiple


def bit_of(index, bit):
    return (index >> bit) & 1


def exchange(value, mask, devices):
    return lax.ppermute(value, AXES, [(d, d ^ mask) for d in range(devices)])


def masks_of(group):
    width = len(group)
    return [
        sum(((t >> (width - 1 - j)) & 1) << group[j] for j in range(width))
        for t in range(1 << width)
    ]


def part_of(index, group):
    return sum(bit_of(index, bit) << (len(group) - 1 - j) for j, bit in enumerate(group))


def reduce_blocks(packed, devices):
    index = lax.axis_index(AXES)
    shards = packed.shape[0]
    pairs = packed.reshape((shards // 2, 2) + packed.shape[1:])
    mine = bit_of(index, CORE_BIT)
    keep = lax.dynamic_index_in_dim(pairs, mine, 1, keepdims=False)
    send = lax.dynamic_index_in_dim(pairs, 1 - mine, 1, keepdims=False)
    blocks = keep + exchange(send, 1 << CORE_BIT, devices)
    mine = part_of(index, Y_GROUP)
    masks = masks_of(Y_GROUP)
    total = lax.dynamic_index_in_dim(blocks, mine, 0, keepdims=False)
    for t in range(1, len(masks)):
        part = lax.dynamic_index_in_dim(blocks, mine ^ t, 0, keepdims=False)
        total = total + exchange(part, masks[t], devices)
    rows, lanes = total.shape
    multiple = ROW_TILE << len(REPLICA_SPLITS)
    total = jnp.pad(total, ((0, padded_width(rows, multiple) - rows), (0, 0)))
    for mask, bit in REPLICA_SPLITS:
        halves = total.reshape((2, total.shape[0] // 2, lanes))
        mine = bit_of(index, bit)
        keep = lax.dynamic_index_in_dim(halves, mine, 0, keepdims=False)
        send = lax.dynamic_index_in_dim(halves, 1 - mine, 0, keepdims=False)
        total = keep + exchange(send, mask, devices)
    for mask in REPLICA_BUTTERFLY:
        total = total + exchange(total, mask, devices)
    for mask, bit in reversed(REPLICA_SPLITS):
        other = exchange(total, mask, devices)
        first = bit_of(index, bit) == 0
        total = jnp.concatenate([jnp.where(first, total, other), jnp.where(first, other, total)], axis=0)
    return total[:rows]


def as_tile(value, rows, lanes):
    if value.size == rows * lanes:
        return value.reshape(rows, lanes)
    flat = value.reshape(1, -1)
    flat = jnp.pad(flat, ((0, 0), (0, lanes * (-(-flat.shape[1] // lanes)) - flat.shape[1])))
    flat = flat.reshape(-1, lanes)
    return jnp.pad(flat, ((0, rows - flat.shape[0]), (0, 0)))


def on_device(
    grad_query,
    grad_output,
    grad_norm,
    grad_bias,
    weight_query,
    weight_output,
    weight_norm,
    weight_bias,
    first_query,
    first_output,
    first_norm,
    first_bias,
    second_query,
    second_output,
    second_norm,
    second_bias,
    shards,
    replicas,
):
    weights = (weight_query, weight_output, weight_norm, weight_bias)
    moments = (first_query, first_output, first_norm, first_bias)
    seconds = (second_query, second_output, second_norm, second_bias)
    decay_rates = (0.01, 0.01, 0.0, 0.0)
    gradients = (grad_query[0], grad_output[0], grad_norm[0], grad_bias[0])
    sizes = [weight.size for weight in weights]
    offsets = [sum(sizes[:member]) for member in range(4)]
    total = sum(sizes)
    devices = shards * replicas
    query_rows, lanes = weight_query.shape
    output_rows = weight_output.size // lanes
    small = jnp.concatenate(
        [grad_norm[0].reshape(shards, -1), grad_bias[0].reshape(shards, -1)], axis=1
    )
    small_width = small.shape[1]
    small = jnp.pad(small, ((0, 0), (0, lanes - small_width))).reshape(shards, 1, lanes)
    small = jnp.pad(small, ((0, 0), (0, 7), (0, 0)))
    packed = jnp.concatenate(
        [
            grad_query[0].reshape(shards, query_rows, lanes),
            grad_output[0].reshape(shards, output_rows, lanes),
            small,
        ],
        axis=1,
    )
    block = reduce_blocks(packed, devices)
    summed_rest = block[query_rows + output_rows, :small_width]
    summed_all = [
        block[:query_rows],
        block[query_rows : query_rows + output_rows].reshape(weight_output.shape),
        summed_rest[: weight_norm.size].reshape(weight_norm.shape),
        summed_rest[weight_norm.size :].reshape(weight_bias.shape),
    ]
    results = [
        step_math(
            summed_all[member],
            moments[member],
            seconds[member],
            weights[member],
            decay_rates[member],
        )
        for member in range(4)
    ]
    terms = [as_tile(weight, query_rows, lanes) for weight in weights]
    terms += [as_tile(result[2], query_rows, lanes) for result in results]
    stacked = jnp.stack(terms)
    squares = lax.psum(jnp.sum(stacked * stacked, axis=(1, 2)), "shard")
    norm_table = jnp.sqrt(squares.reshape(2, -1))
    weight_sizes = norm_table[0]
    update_sizes = norm_table[1]
    trust_ratios = weight_sizes / (update_sizes + 1e-06)
    members = len(weights)
    ratios = (0.01 * trust_ratios).reshape(members, 1, 1)
    updated = (stacked[:members] - ratios * stacked[members:]).astype(jnp.bfloat16)
    norm_size = weight_norm.size
    rest = jnp.concatenate([updated[2, 0, :norm_size], updated[3, 0, : weight_bias.size]])
    rest = jnp.pad(rest, (0, lanes - rest.shape[0])).reshape(1, lanes)
    payload = jnp.concatenate([updated[0], updated[1], rest], axis=0)
    gather_rows = padded_width(payload.shape[0], 2 * ROW_TILE)
    payload = jnp.pad(payload, ((0, gather_rows - payload.shape[0]), (0, 0)))
    gathered = lax.all_gather(payload, "shard", axis=0, tiled=False)
    gathered_rest = gathered[:, query_rows + output_rows]
    full = [
        gathered[:, :query_rows].reshape(-1, lanes),
        gathered[:, query_rows : query_rows + output_rows]
        .reshape((shards,) + weight_output.shape)
        .reshape((-1,) + weight_output.shape[1:]),
        gathered_rest[:, :norm_size].reshape(-1),
        gathered_rest[:, norm_size : norm_size + weight_bias.size]
        .reshape((shards,) + weight_bias.shape)
        .reshape((-1,) + weight_bias.shape[1:]),
    ]
    return (
        full[0],
        full[1],
        full[2],
        full[3],
        results[0][0],
        results[1][0],
        results[2][0],
        results[3][0],
        results[0][1],
        results[1][1],
        results[2][1],
        results[3][1],
        norm_table,
        trust_ratios,
    )


def solution(mesh):
    shards = mesh.shape["shard"]
    replicas = mesh.shape["replica"]
    placed = (
        P(("replica", "shard"), None, None),
        P(("replica", "shard"), None, None),
        P(("replica", "shard"), None),
        P(("replica", "shard"), None, None),
        P("shard", None),
        P("shard", None),
        P("shard"),
        P("shard", None),
        P("shard", None),
        P("shard", None),
        P("shard"),
        P("shard", None),
        P("shard", None),
        P("shard", None),
        P("shard"),
        P("shard", None),
    )

    def body(*args):
        return on_device(*args, shards=shards, replicas=replicas)

    return jax.shard_map(
        body,
        mesh=mesh,
        in_specs=placed,
        out_specs=(
            P(),
            P(),
            P(),
            P(),
            P("shard", None),
            P("shard", None),
            P("shard"),
            P("shard", None),
            P("shard", None),
            P("shard", None),
            P("shard"),
            P("shard", None),
            P(),
            P(),
        ),
        check_vma=False,
    )
```
